512 devices in a mesh: dp: 16 (over z_hi, y), tensor: 32 (over x, z_lo, core).
Axes of the slice: x: 4, y: 8, z: 8 (z_hi: 2, z_lo: 4; z = z_hi * 4 + z_lo), core: 2. Of those that a mesh axis runs over, the one named last changes fastest.
Arguments:
- suffix_states: bfloat16 [32, 128, 2048], P(None, 'dp', 'tensor'), may hold values from -16 to 16
- suffix_lengths: int32 [32], replicated, may hold values from 1 to 128, 2560 in all
- request_group: int32 [32, 1], replicated, may hold values from 0 to 15
- group_owner: int32 [16], replicated, may hold values from 0 to 15, each once
- request_order: int32 [32], replicated, may hold values from 0 to 31, each once
- prefix_cache: bfloat16 [16, 256, 1024], P('dp', 'tensor'), may hold values from -700 to 700
- norm_attn: bfloat16 [2048], replicated, may hold values from 0.099609375 to 1.8984375
- w_query: bfloat16 [2048, 2048], P(None, 'tensor'), may hold values from -0.125 to 0.125
- w_key: bfloat16 [2048, 512], P(None, 'tensor'), may hold values from -0.125 to 0.125
- w_value: bfloat16 [2048, 512], P(None, 'tensor'), may hold values from -0.125 to 0.125
- w_out: bfloat16 [2048, 2048], P('tensor'), may hold values from -0.25 to 0.25
- norm_mlp: bfloat16 [2048], replicated, may hold values from 0.099609375 to 1.8984375
- w_gate: bfloat16 [2048, 8192], P(None, 'tensor'), may hold values from -0.125 to 0.125
- w_up: bfloat16 [2048, 8192], P(None, 'tensor'), may hold values from -0.125 to 0.125
- w_down: bfloat16 [8192, 2048], P('tensor'), may hold values from -0.125 to 0.125
Outputs:
- hidden_out: bfloat16 [32, 128, 2048], P(None, 'dp', 'tensor')
- suffix_keys: bfloat16 [32, 128, 512], P('dp', None, 'tensor')
- suffix_values: bfloat16 [32, 128, 512], P('dp', None, 'tensor')
The draws below stay inside these ranges and needn't reach their ends.
Inputs may be any that keep to these rules, and one draw needn't show every extreme that they name: `suffix_lengths`: the lengths sum to 2560 and some request has exactly 128. `request_group`: every group has at least one request. `group_owner`: A permutation of the 16 groups onto the slots of prefix_cache. `request_order`: A permutation of the requests; slot s belongs to index s // 2 of dp.
All inputs are finite; a program needn't handle non-finite values.
Results may differ from the reference program's by a relative error of at most 0.03.
Values may be sent and summed in bfloat16 or wider, within the bound.
No kernel may reach another device: no remote copies, remote signals or barrier semaphores. Data moves between devices by JAX's collectives and lax.ppermute only.
A program may use at most 64 MiB of HBM per device.

```python
import math
import jax
import jax.numpy as jnp
import numpy as np
from jax import lax

D = 2048
H = 32
KVH = 8
HD = 64
FF = 8192
L_MAX = 128
P_SIZE = 256
REQS = 32
N_DP = 16


def draw_suffix_states(key, part):
    key_scale, key_base = jax.random.split(jax.random.fold_in(key, 11), 2)
    row_scale = jnp.exp(jax.random.uniform(key_scale, (REQS, L_MAX, 1), jnp.float32, math.log(0.4), math.log(4.0)))
    base = jnp.clip(jax.random.normal(key_base, (REQS, L_MAX, D), jnp.float32), -4.0, 4.0)
    return (base * row_scale).astype(jnp.bfloat16)


def draw_prefix_cache(key, part):
    key_base = jax.random.fold_in(jax.random.fold_in(key, 23), 0)
    shape = (N_DP, P_SIZE, KVH * 2 * HD)
    is_key = (jnp.arange(KVH * 2 * HD) % (2 * HD) < HD)[None, None, :]
    value_gain = jnp.where(is_key, 1.0, 8.0)
    values = jnp.clip(jax.random.normal(key_base, shape, jnp.float32), -4.0, 4.0) * value_gain
    return values.astype(jnp.bfloat16)


def strengthened(drawn, key, source, target, parts, factor):
    owner, partner = [(jnp.arange(drawn.shape[dim]) // (drawn.shape[dim] // parts)).reshape([-1 if axis == dim else 1 for axis in range(drawn.ndim)]) for dim in (source, target)]
    chosen = jax.random.permutation(key, parts)[partner]
    strong = (owner == chosen) | (owner == (partner + parts // 2) % parts)
    return jnp.where(strong, factor * drawn, drawn)


def block_levels(own_key, extent, pieces, least, high):
    level = 1.0
    for axis_at, parts in pieces:
        steps = jax.random.uniform(jax.random.fold_in(jax.random.fold_in(own_key, 6), axis_at), (parts,), jnp.float32, least / len(pieces), high / len(pieces))
        level = level * jnp.repeat(jnp.exp(steps), extent[axis_at] // parts).reshape((-1,) + (1,) * (len(extent) - 1 - axis_at))
    return level


def picks_of(own_key, rows, number_of, top, lift):
    order = jax.random.permutation(jax.random.fold_in(own_key, 1), number_of)
    boost = order
    for power in range(3):
        boost = boost * boost // number_of
    boost = boost * lift // number_of
    chance = jax.random.randint(jax.random.fold_in(own_key, 2), (rows, number_of), 0, 4096) + boost
    holders = jax.random.permutation(jax.random.fold_in(own_key, 3), rows)[jnp.arange(number_of) % rows]
    chance = jnp.where(jnp.arange(rows)[:, None] == holders[None, :], 1 << 14, chance)
    priority = chance * number_of + jnp.arange(number_of)
    return lax.top_k(priority.astype(jnp.int32), top)[1].astype(jnp.int32)


def profile(amount, total, most, lean):
    loads = [(1 << 20) // math.isqrt(grade ** lean) + 1 for grade in range(2, amount + 1)]
    rest, given = total - most - (amount - 1), [1] * (amount - 1)
    while rest > 0:
        candidates = [i for i in range(amount - 1) if given[i] < most]
        whole, left = sum([loads[i] for i in candidates]), rest
        for i in candidates:
            more = min(most - given[i], max(1, left * loads[i] // whole), rest)
            given[i] = given[i] + more
            rest = rest - more
    return np.array([most] + given)


def ragged_sizes(rng, amount, total, reach, lean):
    if amount == 2:
        one = jax.random.randint(rng, (), max(1, total - reach), min(reach, total - 1) + 1)
        return jnp.stack([one, total - one])
    sizes = jnp.asarray(profile(amount, total, reach, lean), jnp.int32)
    twos = (amount - 1) // 2
    giver, taker = sizes[1:1 + 2 * twos:2], sizes[2:2 + 2 * twos:2]
    margin = jnp.minimum(giver - 1, reach - taker)
    moved = jax.random.randint(jax.random.fold_in(rng, 1), (twos,), 0, 1 << 20) % (margin + 1)
    sizes = sizes.at[1:1 + 2 * twos:2].set(giver - moved).at[2:2 + 2 * twos:2].set(taker + moved)
    return sizes[jax.random.permutation(jax.random.fold_in(rng, 2), amount)]


def scatter_about(own_key, dims, scale, reach, cuts=(), kind=jnp.bfloat16):
    values = jax.random.normal(own_key, dims, jnp.float32) * scale
    if len(cuts) > 0:
        values = block_levels(own_key, dims, cuts, -0.22, 0.18) * values
    return jnp.clip(values, min=-reach, max=reach).astype(kind)


def gaussian_with(own_key, shape, spread, most, cuts, heavy, kind=jnp.bfloat16):
    array = spread * jax.random.normal(own_key, shape, jnp.float32)
    if cuts:
        array = array * block_levels(own_key, shape, cuts, -0.22, 0.18)
    return jnp.clip(strengthened(array, jax.random.fold_in(own_key, 3), *heavy), -most, most).astype(kind)


def setup_inputs(seed: int = 0) -> dict:
    key_of = jax.random.split(jax.random.key(seed), 16)
    return {
        "suffix_states": draw_suffix_states(jax.random.fold_in(key_of[15], 71), 0),
        "suffix_lengths": ragged_sizes(key_of[1], REQS, REQS * L_MAX * 5 // 8, L_MAX, 2).astype(jnp.int32),
        "request_group": picks_of(key_of[2], REQS, N_DP, 1, 512),
        "group_owner": jax.random.permutation(key_of[3], N_DP).astype(jnp.int32),
        "request_order": jax.random.permutation(key_of[4], REQS).astype(jnp.int32),
        "prefix_cache": draw_prefix_cache(jax.random.fold_in(key_of[15], 71), 0),
        "norm_attn": jnp.clip(1.0 + 0.18 * jax.random.normal(key_of[6], (D,), jnp.float32), 0.099609375, 1.8984375).astype(jnp.bfloat16),
        "w_query": scatter_about(key_of[7], (D, H * HD), D ** -0.5, 0.125, ((1, 32),)),
        "w_key": scatter_about(key_of[8], (D, KVH * HD), D ** -0.5, 0.125, ((1, 32),)),
        "w_value": scatter_about(key_of[9], (D, KVH * HD), D ** -0.5, 0.125, ((1, 32),)),
        "w_out": gaussian_with(key_of[10], (H * HD, D), (H * HD) ** -0.5, 0.25, ((0, 32),), (0, 1, 32, 2.75)),
        "norm_mlp": jnp.clip(1.0 + 0.18 * jax.random.normal(key_of[11], (D,), jnp.float32), 0.099609375, 1.8984375).astype(jnp.bfloat16),
        "w_gate": scatter_about(key_of[12], (D, FF), D ** -0.5, 0.125, ((1, 32),)),
        "w_up": scatter_about(key_of[13], (D, FF), D ** -0.5, 0.125, ((1, 32),)),
        "w_down": gaussian_with(key_of[14], (FF, D), FF ** -0.5, 0.125, ((0, 32),), (0, 1, 32, 2.75)),
    }


THETA = 10000000.0
EPSILON = 1e-05

def rms_scale(states, gain):
    wide = states.astype(jnp.float32)
    mean_square = lax.optimization_barrier(jnp.mean(wide * wide, axis=-1, keepdims=True))
    return (wide * lax.rsqrt(mean_square + EPSILON) * gain.astype(jnp.float32)).astype(jnp.bfloat16)

def rotate(vectors, positions):
    half = HD // 2
    freqs = THETA ** (-(jnp.arange(half, dtype=jnp.float32) * 2.0 / HD))
    angles = positions[:, None] * freqs[None, :]
    cosine = jnp.cos(angles)[:, None, :]
    sine = jnp.sin(angles)[:, None, :]
    first = vectors[..., :half]
    second = vectors[..., half:]
    return jnp.concatenate([first * cosine - second * sine, second * cosine + first * sine], axis=-1)

def reference(suffix_states, suffix_lengths, request_group, group_owner, request_order, prefix_cache, norm_attn, w_query, w_key, w_value, w_out, norm_mlp, w_gate, w_up, w_down):
    group_size = H // KVH
    head_map = jnp.arange(H) // group_size
    position = jnp.arange(L_MAX, dtype=jnp.int32)
    positions = (P_SIZE + position).astype(jnp.float32)

    def one_request(index):
        states = suffix_states[index]
        length = suffix_lengths[index]
        owner = group_owner[request_group[index, 0]]
        valid = position < length
        normed = rms_scale(states, norm_attn)
        query = rotate(jnp.dot(normed, w_query, preferred_element_type=jnp.float32).reshape(L_MAX, H, HD), positions).astype(jnp.bfloat16)
        key_part = jnp.dot(normed, w_key, preferred_element_type=jnp.float32).astype(jnp.bfloat16)
        value_part = jnp.dot(normed, w_value, preferred_element_type=jnp.float32).astype(jnp.bfloat16)
        key_heads = key_part.reshape(L_MAX, HD, KVH).transpose(0, 2, 1)
        value_heads = value_part.reshape(L_MAX, HD, KVH).transpose(0, 2, 1)
        key_rot = rotate(key_heads.astype(jnp.float32), positions).astype(jnp.bfloat16)
        cached = lax.dynamic_index_in_dim(prefix_cache, owner, 0, keepdims=False).reshape(P_SIZE, KVH, 2, HD)
        all_keys = jnp.concatenate([cached[:, head_map, 0], key_rot[:, head_map]], axis=0)
        all_values = jnp.concatenate([cached[:, head_map, 1], value_heads[:, head_map]], axis=0)
        scores = jnp.einsum('thd,khd->htk', query.astype(jnp.float32), all_keys.astype(jnp.float32)) * HD ** (-0.5)
        self_allowed = (position[None, :] <= position[:, None]) & (position[None, :] < length)
        allowed = jnp.concatenate([jnp.ones((L_MAX, P_SIZE), dtype=bool), self_allowed], axis=1)[None]
        row_peak = lax.optimization_barrier(jnp.max(jnp.where(allowed, scores, -jnp.inf), axis=2, keepdims=True))
        weights = jnp.where(allowed, jnp.exp(scores - row_peak), 0.0)
        weight_sum = lax.optimization_barrier(jnp.sum(weights, axis=2))
        numerator = jnp.einsum('htk,khd->htd', weights.astype(jnp.bfloat16).astype(jnp.float32), all_values.astype(jnp.float32))
        attention = (numerator / weight_sum[..., None]).astype(jnp.bfloat16)
        attention = attention.transpose(1, 0, 2).reshape(L_MAX, H * HD)
        middle = (states.astype(jnp.float32) + jnp.dot(attention, w_out, preferred_element_type=jnp.float32)).astype(jnp.bfloat16)
        normed_two = rms_scale(middle, norm_mlp)
        gate = jnp.dot(normed_two, w_gate, preferred_element_type=jnp.float32)
        upper = jnp.dot(normed_two, w_up, preferred_element_type=jnp.float32)
        hidden = (jax.nn.silu(gate) * upper).astype(jnp.bfloat16)
        result = middle.astype(jnp.float32) + jnp.dot(hidden, w_down, preferred_element_type=jnp.float32)
        result = jnp.where(valid[:, None], result, 0.0).astype(jnp.bfloat16)
        keys_flat = jnp.where(valid[:, None], key_rot.reshape(L_MAX, KVH * HD), 0.0).astype(jnp.bfloat16)
        values_flat = jnp.where(valid[:, None], value_heads.reshape(L_MAX, KVH * HD), 0.0).astype(jnp.bfloat16)
        return (result, keys_flat, values_flat)
    outputs, key_rows, value_rows = lax.map(one_request, jnp.arange(REQS, dtype=jnp.int32))
    return (outputs, jnp.take(key_rows, request_order, axis=0), jnp.take(value_rows, request_order, axis=0))
```

```python
import jax
import jax.numpy as jnp
import numpy as np
from jax import lax
from jax.sharding import PartitionSpec as P

H = 32
KVH = 8
HD = 64
L_MAX = 128
P_SIZE = 256


THETA = 10000000.0
EPSILON = 1e-05


def rms_scale(wide, gain):
    mean_square = jnp.mean(wide * wide, axis=-1, keepdims=True)
    return (wide * lax.rsqrt(mean_square + EPSILON) * gain.astype(jnp.float32)).astype(jnp.bfloat16)


def rotate(vectors, positions):
    half = HD // 2
    freqs = THETA ** (-(jnp.arange(half, dtype=jnp.float32) * 2.0 / HD))
    angles = positions[:, None] * freqs[None, :]
    cosine = jnp.cos(angles)
    sine = jnp.sin(angles)
    first = vectors[..., :half]
    second = vectors[..., half:]
    return jnp.concatenate(
        [first * cosine - second * sine, second * cosine + first * sine], axis=-1
    )


def gather_rows(shard, axis_name, count):
    sent = jnp.broadcast_to(shard[None], (count,) + shard.shape)
    got = lax.all_to_all(sent, axis_name, 0, 0, tiled=True)
    rows, width = shard.shape
    return got.transpose(1, 0, 2).reshape(rows, count * width)


def scatter_sum(terms, axis_name, count):
    rows, width = terms.shape
    share = width // count
    sent = terms.astype(jnp.bfloat16).reshape(rows, count, share).transpose(1, 0, 2)
    got = lax.all_to_all(sent, axis_name, 0, 0, tiled=True)
    return jnp.sum(got.astype(jnp.float32), axis=0)


def shards(
    suffix_states,
    suffix_lengths,
    request_group,
    group_owner,
    request_order,
    prefix_cache,
    norm_attn,
    w_query,
    w_key,
    w_value,
    w_out,
    norm_mlp,
    w_gate,
    w_up,
    w_down,
):
    dp_count = lax.axis_size("dp")
    tp_count = lax.axis_size("tensor")
    dp_index = lax.axis_index("dp")
    tp_index = lax.axis_index("tensor")
    total_reqs = suffix_lengths.shape[0]
    local_reqs = total_reqs // dp_count
    row_count = local_reqs * L_MAX
    heads_here = w_query.shape[1] // HD
    group_size = H // KVH
    assert heads_here == 1
    kv_cols = w_key.shape[1]
    d_here = kv_cols // KVH
    score_scale = HD ** (-0.5)
    kv_of_dest = np.arange(tp_count) * heads_here // group_size
    kv_here = tp_index * heads_here // group_size

    col_pick = (np.arange(d_here)[None, :] * KVH + kv_of_dest[:, None]).reshape(-1)
    w_pair = jnp.concatenate([w_key, w_value], axis=1)
    pick = np.concatenate([col_pick.reshape(tp_count, d_here), kv_cols + col_pick.reshape(tp_count, d_here)], axis=1)
    w_sent = jnp.take(w_pair, pick.reshape(-1), axis=1).reshape(w_key.shape[0], tp_count, 2 * d_here)
    w_got = lax.all_to_all(w_sent.transpose(1, 0, 2), "tensor", 0, 0, tiled=True)
    k_head_w = w_got[:, :, :d_here].transpose(1, 0, 2).reshape(w_key.shape[0], HD)
    v_head_w = w_got[:, :, d_here:].transpose(1, 0, 2).reshape(w_key.shape[0], HD)

    routed = jnp.take(suffix_states, request_order, axis=0)
    pos_here = routed.shape[1]
    width_here = routed.shape[2]
    state_part = routed.reshape(dp_count, local_reqs * pos_here * width_here)
    prefix_flat = prefix_cache.reshape(1, -1)
    prefix_part = jnp.broadcast_to(prefix_flat, (dp_count, prefix_flat.shape[1]))
    first = lax.all_to_all(
        jnp.concatenate([state_part, prefix_part], axis=1), "dp", 0, 0, tiled=True
    )
    state_split = state_part.shape[1]
    routed_here = (
        first[:, :state_split]
        .reshape(dp_count, local_reqs, pos_here, width_here)
        .transpose(1, 0, 2, 3)
        .reshape(local_reqs, dp_count * pos_here, width_here)
    )
    prefix_rows = prefix_cache.shape[1]
    prefix_all = first[:, state_split:].reshape(dp_count, prefix_rows, KVH, 2 * HD)

    state_shard = routed_here.reshape(row_count, width_here)
    slot_ids = dp_index * local_reqs + jnp.arange(local_reqs, dtype=jnp.int32)
    req_ids = jnp.take(request_order, slot_ids)
    lengths_here = jnp.take(suffix_lengths, req_ids)
    owner_here = jnp.take(group_owner, jnp.take(request_group[:, 0], req_ids))
    position = jnp.arange(L_MAX, dtype=jnp.int32)
    valid = (position[None, :] < lengths_here[:, None]).reshape(row_count)
    positions = (P_SIZE + position).astype(jnp.float32)

    chosen = jnp.take(prefix_all, owner_here, axis=0)
    chosen = jnp.take(chosen, kv_of_dest, axis=2).transpose(2, 0, 1, 3)
    picked = lax.all_to_all(chosen, "tensor", 0, 0, tiled=True)
    picked = picked.transpose(1, 0, 2, 3).reshape(local_reqs, tp_count * prefix_rows, 2 * HD)
    prefix_keys = picked[:, :, :HD]
    prefix_values = picked[:, :, HD:]

    full_rows = gather_rows(state_shard, "tensor", tp_count)
    normed = rms_scale(full_rows.astype(jnp.float32), norm_attn)
    query = jnp.dot(normed, w_query, preferred_element_type=jnp.float32).reshape(
        local_reqs, L_MAX, HD
    )
    query = rotate(query, positions).astype(jnp.bfloat16)
    key_raw = jnp.dot(normed, k_head_w, preferred_element_type=jnp.float32).astype(jnp.bfloat16)
    value = jnp.dot(normed, v_head_w, preferred_element_type=jnp.float32).astype(jnp.bfloat16)
    key_rot = rotate(
        key_raw.reshape(local_reqs, L_MAX, HD).astype(jnp.float32), positions
    ).astype(jnp.bfloat16)
    value = value.reshape(local_reqs, L_MAX, HD)

    valid3 = valid.reshape(local_reqs, L_MAX, 1)
    out_width = kv_cols
    out_first = (tp_index * out_width) % HD
    keys_out = jnp.where(
        valid3, lax.dynamic_slice_in_dim(key_rot, out_first, out_width, 2), 0.0
    ).astype(jnp.bfloat16)
    values_out = jnp.where(
        valid3, lax.dynamic_slice_in_dim(value, out_first, out_width, 2), 0.0
    ).astype(jnp.bfloat16)

    prefix_scores = jnp.einsum(
        "rtd,rpd->rtp", query, prefix_keys, preferred_element_type=jnp.float32
    ) * score_scale
    self_scores = jnp.einsum(
        "rtd,rsd->rts", query, key_rot, preferred_element_type=jnp.float32
    ) * score_scale
    self_allowed = (position[None, None, :] <= position[None, :, None]) & (
        position[None, None, :] < lengths_here[:, None, None]
    )
    scores = jnp.concatenate([prefix_scores, self_scores], axis=2)
    allowed = jnp.concatenate(
        [jnp.ones(prefix_scores.shape, bool), self_allowed], axis=2
    )
    row_peak = jnp.max(jnp.where(allowed, scores, -jnp.inf), axis=2, keepdims=True)
    weights = jnp.where(allowed, jnp.exp(scores - row_peak), 0.0)
    total = jnp.sum(weights, axis=2, keepdims=True)
    all_values = jnp.concatenate([prefix_values, value], axis=1)
    numerator = jnp.einsum(
        "rtk,rkd->rtd", weights.astype(jnp.bfloat16), all_values, preferred_element_type=jnp.float32
    )
    attention = (numerator / total).astype(jnp.bfloat16).reshape(row_count, HD)

    attn_terms = jnp.dot(attention, w_out, preferred_element_type=jnp.float32)
    attn_share = scatter_sum(attn_terms, "tensor", tp_count)
    middle = (state_shard.astype(jnp.float32) + attn_share).astype(jnp.bfloat16)
    middle_rows = gather_rows(middle, "tensor", tp_count)
    normed_two = rms_scale(middle_rows.astype(jnp.float32), norm_mlp)
    gate = jnp.dot(normed_two, w_gate, preferred_element_type=jnp.float32)
    upper = jnp.dot(normed_two, w_up, preferred_element_type=jnp.float32)
    hidden = (jax.nn.silu(gate) * upper).astype(jnp.bfloat16)
    down_terms = jnp.dot(hidden, w_down, preferred_element_type=jnp.float32)
    down_share = scatter_sum(down_terms, "tensor", tp_count)
    result = middle.astype(jnp.float32) + down_share
    result = (
        jnp.where(valid[:, None], result, 0.0)
        .astype(jnp.bfloat16)
        .reshape(local_reqs, L_MAX, width_here)
    )
    returned = lax.all_to_all(result, "dp", split_axis=1, concat_axis=0, tiled=True)
    hidden_out = jnp.zeros_like(returned).at[request_order].set(returned)
    return (hidden_out, keys_out, values_out)


def solution(mesh):
    in_specs = (
        P(None, "dp", "tensor"),
        P(),
        P(),
        P(),
        P(),
        P("dp", "tensor", None),
        P(),
        P(None, "tensor"),
        P(None, "tensor"),
        P(None, "tensor"),
        P("tensor", None),
        P(),
        P(None, "tensor"),
        P(None, "tensor"),
        P("tensor", None),
    )
    out_specs = (P(None, "dp", "tensor"), P("dp", None, "tensor"), P("dp", None, "tensor"))
    return jax.shard_map(shards, mesh=mesh, in_specs=in_specs, out_specs=out_specs, check_vma=False)
```

```python
import jax
import jax.numpy as jnp
import numpy as np
from jax import lax
from jax.sharding import PartitionSpec as P

H = 32
KVH = 8
HD = 64
L_MAX = 128
P_SIZE = 256


THETA = 10000000.0
EPSILON = 1e-05


def rms_scale(wide, gain):
    mean_square = jnp.mean(wide * wide, axis=-1, keepdims=True)
    return (wide * lax.rsqrt(mean_square + EPSILON) * gain.astype(jnp.float32)).astype(jnp.bfloat16)


def rotate(vectors, positions):
    half = HD // 2
    freqs = THETA ** (-(jnp.arange(half, dtype=jnp.float32) * 2.0 / HD))
    angles = positions[:, None] * freqs[None, :]
    cosine = jnp.cos(angles)
    sine = jnp.sin(angles)
    first = vectors[..., :half]
    second = vectors[..., half:]
    return jnp.concatenate(
        [first * cosine - second * sine, second * cosine + first * sine], axis=-1
    )


def gather_rows(shard, axis_name, count):
    sent = jnp.broadcast_to(shard[None], (count,) + shard.shape)
    got = lax.all_to_all(sent, axis_name, 0, 0, tiled=True)
    rows, width = shard.shape
    return got.transpose(1, 0, 2).reshape(rows, count * width)


def scatter_sum(terms, axis_name, count):
    rows, width = terms.shape
    share = width // count
    sent = terms.astype(jnp.bfloat16).reshape(rows, count, share).transpose(1, 0, 2)
    got = lax.all_to_all(sent, axis_name, 0, 0, tiled=True)
    return jnp.sum(got.astype(jnp.float32), axis=0)


def shards(
    suffix_states,
    suffix_lengths,
    request_group,
    group_owner,
    request_order,
    prefix_cache,
    norm_attn,
    w_query,
    w_key,
    w_value,
    w_out,
    norm_mlp,
    w_gate,
    w_up,
    w_down,
):
    dp_count = lax.axis_size("dp")
    tp_count = lax.axis_size("tensor")
    dp_index = lax.axis_index("dp")
    tp_index = lax.axis_index("tensor")
    total_reqs = suffix_lengths.shape[0]
    local_reqs = total_reqs // dp_count
    row_count = local_reqs * L_MAX
    heads_here = w_query.shape[1] // HD
    group_size = H // KVH
    assert heads_here == 1
    kv_cols = w_key.shape[1]
    d_here = kv_cols // KVH
    score_scale = HD ** (-0.5)
    kv_of_dest = np.arange(tp_count) * heads_here // group_size
    kv_here = tp_index * heads_here // group_size

    col_pick = (np.arange(d_here)[None, :] * KVH + kv_of_dest[:, None]).reshape(-1)
    w_pair = jnp.concatenate([w_key, w_value], axis=1)
    pick = np.concatenate([col_pick.reshape(tp_count, d_here), kv_cols + col_pick.reshape(tp_count, d_here)], axis=1)
    w_sent = jnp.take(w_pair, pick.reshape(-1), axis=1).reshape(w_key.shape[0], tp_count, 2 * d_here)
    w_sent = w_sent.transpose(1, 0, 2).reshape(tp_count, -1)

    routed = jnp.take(suffix_states, request_order, axis=0)
    pos_here = routed.shape[1]
    width_here = routed.shape[2]
    state_part = routed.reshape(dp_count, local_reqs * pos_here * width_here)
    prefix_flat = prefix_cache.reshape(1, -1)
    prefix_part = jnp.broadcast_to(prefix_flat, (dp_count, prefix_flat.shape[1]))
    first = lax.all_to_all(
        jnp.concatenate([state_part, prefix_part], axis=1), "dp", 0, 0, tiled=True
    )
    state_split = state_part.shape[1]
    routed_here = (
        first[:, :state_split]
        .reshape(dp_count, local_reqs, pos_here, width_here)
        .transpose(1, 0, 2, 3)
        .reshape(local_reqs, dp_count * pos_here, width_here)
    )
    prefix_rows = prefix_cache.shape[1]
    prefix_all = first[:, state_split:].reshape(dp_count, prefix_rows, KVH, 2 * HD)

    state_shard = routed_here.reshape(row_count, width_here)
    slot_ids = dp_index * local_reqs + jnp.arange(local_reqs, dtype=jnp.int32)
    req_ids = jnp.take(request_order, slot_ids)
    lengths_here = jnp.take(suffix_lengths, req_ids)
    owner_here = jnp.take(group_owner, jnp.take(request_group[:, 0], req_ids))
    position = jnp.arange(L_MAX, dtype=jnp.int32)
    valid = (position[None, :] < lengths_here[:, None]).reshape(row_count)
    positions = (P_SIZE + position).astype(jnp.float32)

    chosen = jnp.take(prefix_all, owner_here, axis=0)
    chosen = jnp.take(chosen, kv_of_dest, axis=2).transpose(2, 0, 1, 3)
    state_sent = jnp.broadcast_to(state_shard.reshape(1, -1), (tp_count, row_count * width_here))
    prefix_sent = chosen.reshape(tp_count, -1)
    cuts = np.cumsum([state_sent.shape[1], prefix_sent.shape[1]])
    got = lax.all_to_all(
        jnp.concatenate([state_sent, prefix_sent, w_sent], axis=1), "tensor", 0, 0, tiled=True
    )
    full_rows = (
        got[:, : cuts[0]].reshape(tp_count, row_count, width_here)
        .transpose(1, 0, 2).reshape(row_count, tp_count * width_here)
    )
    picked = got[:, cuts[0] : cuts[1]].reshape(tp_count, local_reqs, prefix_rows, 2 * HD)
    picked = picked.transpose(1, 0, 2, 3).reshape(local_reqs, tp_count * prefix_rows, 2 * HD)
    prefix_keys = picked[:, :, :HD]
    prefix_values = picked[:, :, HD:]
    w_got = got[:, cuts[1] :].reshape(tp_count, w_key.shape[0], 2 * d_here)
    k_head_w = w_got[:, :, :d_here].transpose(1, 0, 2).reshape(w_key.shape[0], HD)
    v_head_w = w_got[:, :, d_here:].transpose(1, 0, 2).reshape(w_key.shape[0], HD)

    normed = rms_scale(full_rows.astype(jnp.float32), norm_attn)
    query = jnp.dot(normed, w_query, preferred_element_type=jnp.float32).reshape(
        local_reqs, L_MAX, HD
    )
    query = rotate(query, positions).astype(jnp.bfloat16)
    key_raw = jnp.dot(normed, k_head_w, preferred_element_type=jnp.float32).astype(jnp.bfloat16)
    value = jnp.dot(normed, v_head_w, preferred_element_type=jnp.float32).astype(jnp.bfloat16)
    key_rot = rotate(
        key_raw.reshape(local_reqs, L_MAX, HD).astype(jnp.float32), positions
    ).astype(jnp.bfloat16)
    value = value.reshape(local_reqs, L_MAX, HD)

    valid3 = valid.reshape(local_reqs, L_MAX, 1)
    out_width = kv_cols
    out_first = (tp_index * out_width) % HD
    keys_out = jnp.where(
        valid3, lax.dynamic_slice_in_dim(key_rot, out_first, out_width, 2), 0.0
    ).astype(jnp.bfloat16)
    values_out = jnp.where(
        valid3, lax.dynamic_slice_in_dim(value, out_first, out_width, 2), 0.0
    ).astype(jnp.bfloat16)

    prefix_scores = jnp.einsum(
        "rtd,rpd->rtp", query, prefix_keys, preferred_element_type=jnp.float32
    ) * score_scale
    self_scores = jnp.einsum(
        "rtd,rsd->rts", query, key_rot, preferred_element_type=jnp.float32
    ) * score_scale
    self_allowed = (position[None, None, :] <= position[None, :, None]) & (
        position[None, None, :] < lengths_here[:, None, None]
    )
    scores = jnp.concatenate([prefix_scores, self_scores], axis=2)
    allowed = jnp.concatenate(
        [jnp.ones(prefix_scores.shape, bool), self_allowed], axis=2
    )
    row_peak = jnp.max(jnp.where(allowed, scores, -jnp.inf), axis=2, keepdims=True)
    weights = jnp.where(allowed, jnp.exp(scores - row_peak), 0.0)
    total = jnp.sum(weights, axis=2, keepdims=True)
    all_values = jnp.concatenate([prefix_values, value], axis=1)
    numerator = jnp.einsum(
        "rtk,rkd->rtd", weights.astype(jnp.bfloat16), all_values, preferred_element_type=jnp.float32
    )
    attention = (numerator / total).astype(jnp.bfloat16).reshape(row_count, HD)

    attn_terms = jnp.dot(attention, w_out, preferred_element_type=jnp.float32)
    attn_share = scatter_sum(attn_terms, "tensor", tp_count)
    middle = (state_shard.astype(jnp.float32) + attn_share).astype(jnp.bfloat16)
    middle_rows = gather_rows(middle, "tensor", tp_count)
    normed_two = rms_scale(middle_rows.astype(jnp.float32), norm_mlp)
    gate = jnp.dot(normed_two, w_gate, preferred_element_type=jnp.float32)
    upper = jnp.dot(normed_two, w_up, preferred_element_type=jnp.float32)
    hidden = (jax.nn.silu(gate) * upper).astype(jnp.bfloat16)
    down_terms = jnp.dot(hidden, w_down, preferred_element_type=jnp.float32)
    down_share = scatter_sum(down_terms, "tensor", tp_count)
    result = middle.astype(jnp.float32) + down_share
    result = (
        jnp.where(valid[:, None], result, 0.0)
        .astype(jnp.bfloat16)
        .reshape(local_reqs, L_MAX, width_here)
    )
    returned = lax.all_to_all(result, "dp", split_axis=1, concat_axis=0, tiled=True)
    hidden_out = jnp.zeros_like(returned).at[request_order].set(returned)
    return (hidden_out, keys_out, values_out)


def solution(mesh):
    in_specs = (
        P(None, "dp", "tensor"),
        P(),
        P(),
        P(),
        P(),
        P("dp", "tensor", None),
        P(),
        P(None, "tensor"),
        P(None, "tensor"),
        P(None, "tensor"),
        P("tensor", None),
        P(),
        P(None, "tensor"),
        P(None, "tensor"),
        P("tensor", None),
    )
    out_specs = (P(None, "dp", "tensor"), P("dp", None, "tensor"), P("dp", None, "tensor"))
    return jax.shard_map(shards, mesh=mesh, in_specs=in_specs, out_specs=out_specs, check_vma=False)
```

```python
import jax
import jax.numpy as jnp
import numpy as np
from jax import lax
from jax.sharding import PartitionSpec as P

H = 32
KVH = 8
HD = 64
L_MAX = 128
P_SIZE = 256


THETA = 10000000.0
EPSILON = 1e-05


def rms_scale(wide, gain):
    mean_square = jnp.mean(wide * wide, axis=-1, keepdims=True)
    return (wide * lax.rsqrt(mean_square + EPSILON) * gain.astype(jnp.float32)).astype(jnp.bfloat16)


def rotate(vectors, positions):
    half = HD // 2
    freqs = THETA ** (-(jnp.arange(half, dtype=jnp.float32) * 2.0 / HD))
    angles = positions[:, None] * freqs[None, :]
    cosine = jnp.cos(angles)
    sine = jnp.sin(angles)
    first = vectors[..., :half]
    second = vectors[..., half:]
    return jnp.concatenate(
        [first * cosine - second * sine, second * cosine + first * sine], axis=-1
    )


def gather_rows(shard, axis_name, count):
    sent = jnp.broadcast_to(shard[None], (count,) + shard.shape)
    got = lax.all_to_all(sent, axis_name, 0, 0, tiled=True)
    rows, width = shard.shape
    return got.transpose(1, 0, 2).reshape(rows, count * width)


def scatter_sum(terms, axis_name, count):
    rows, width = terms.shape
    share = width // count
    sent = terms.astype(jnp.bfloat16).reshape(rows, count, share).transpose(1, 0, 2)
    got = lax.all_to_all(sent, axis_name, 0, 0, tiled=True)
    return jnp.sum(got.astype(jnp.float32), axis=0)


def shards(
    suffix_states,
    suffix_lengths,
    request_group,
    group_owner,
    request_order,
    prefix_cache,
    norm_attn,
    w_query,
    w_key,
    w_value,
    w_out,
    norm_mlp,
    w_gate,
    w_up,
    w_down,
):
    dp_count = lax.axis_size("dp")
    tp_count = lax.axis_size("tensor")
    dp_index = lax.axis_index("dp")
    tp_index = lax.axis_index("tensor")
    total_reqs = suffix_lengths.shape[0]
    local_reqs = total_reqs // dp_count
    row_count = local_reqs * L_MAX
    heads_here = w_query.shape[1] // HD
    group_size = H // KVH
    assert heads_here == 1
    kv_cols = w_key.shape[1]
    d_here = kv_cols // KVH
    score_scale = HD ** (-0.5)
    kv_of_dest = np.arange(tp_count) * heads_here // group_size
    kv_here = tp_index * heads_here // group_size

    routed = jnp.take(suffix_states, request_order, axis=0)
    pos_here = routed.shape[1]
    width_here = routed.shape[2]
    state_part = routed.reshape(dp_count, local_reqs * pos_here * width_here)
    prefix_flat = prefix_cache.reshape(1, -1)
    prefix_part = jnp.broadcast_to(prefix_flat, (dp_count, prefix_flat.shape[1]))
    first = lax.all_to_all(
        jnp.concatenate([state_part, prefix_part], axis=1), "dp", 0, 0, tiled=True
    )
    state_split = state_part.shape[1]
    routed_here = (
        first[:, :state_split]
        .reshape(dp_count, local_reqs, pos_here, width_here)
        .transpose(1, 0, 2, 3)
        .reshape(local_reqs, dp_count * pos_here, width_here)
    )
    prefix_rows = prefix_cache.shape[1]
    prefix_all = first[:, state_split:].reshape(dp_count, prefix_rows, KVH, 2 * HD)

    state_shard = routed_here.reshape(row_count, width_here)
    slot_ids = dp_index * local_reqs + jnp.arange(local_reqs, dtype=jnp.int32)
    req_ids = jnp.take(request_order, slot_ids)
    lengths_here = jnp.take(suffix_lengths, req_ids)
    owner_here = jnp.take(group_owner, jnp.take(request_group[:, 0], req_ids))
    position = jnp.arange(L_MAX, dtype=jnp.int32)
    valid = (position[None, :] < lengths_here[:, None]).reshape(row_count)
    positions = (P_SIZE + position).astype(jnp.float32)

    chosen = jnp.take(prefix_all, owner_here, axis=0)
    chosen = jnp.take(chosen, kv_of_dest, axis=2).transpose(2, 0, 1, 3)
    picked = lax.all_to_all(chosen, "tensor", 0, 0, tiled=True)
    picked = picked.transpose(1, 0, 2, 3).reshape(local_reqs, tp_count * prefix_rows, 2 * HD)
    prefix_keys = picked[:, :, :HD]
    prefix_values = picked[:, :, HD:]

    full_rows = gather_rows(state_shard, "tensor", tp_count)
    normed = rms_scale(full_rows.astype(jnp.float32), norm_attn)
    query = jnp.dot(normed, w_query, preferred_element_type=jnp.float32).reshape(
        local_reqs, L_MAX, HD
    )
    query = rotate(query, positions).astype(jnp.bfloat16)
    kv_part = jnp.dot(
        normed, jnp.concatenate([w_key, w_value], axis=1), preferred_element_type=jnp.float32
    ).astype(jnp.bfloat16)
    pick = (np.arange(d_here)[None, :] * KVH + kv_of_dest[:, None])
    pick = np.concatenate([pick, kv_cols + pick], axis=1)
    kv_sent = jnp.take(kv_part, pick.reshape(-1), axis=1).reshape(row_count, tp_count, 2 * d_here)
    kv_got = lax.all_to_all(kv_sent.transpose(1, 0, 2), "tensor", 0, 0, tiled=True)
    key_raw = kv_got[:, :, :d_here].transpose(1, 0, 2).reshape(row_count, HD)
    value = kv_got[:, :, d_here:].transpose(1, 0, 2).reshape(row_count, HD)
    key_rot = rotate(
        key_raw.reshape(local_reqs, L_MAX, HD).astype(jnp.float32), positions
    ).astype(jnp.bfloat16)
    value = value.reshape(local_reqs, L_MAX, HD)

    valid3 = valid.reshape(local_reqs, L_MAX, 1)
    out_width = kv_cols
    out_first = (tp_index * out_width) % HD
    keys_out = jnp.where(
        valid3, lax.dynamic_slice_in_dim(key_rot, out_first, out_width, 2), 0.0
    ).astype(jnp.bfloat16)
    values_out = jnp.where(
        valid3, lax.dynamic_slice_in_dim(value, out_first, out_width, 2), 0.0
    ).astype(jnp.bfloat16)

    prefix_scores = jnp.einsum(
        "rtd,rpd->rtp", query, prefix_keys, preferred_element_type=jnp.float32
    ) * score_scale
    self_scores = jnp.einsum(
        "rtd,rsd->rts", query, key_rot, preferred_element_type=jnp.float32
    ) * score_scale
    self_allowed = (position[None, None, :] <= position[None, :, None]) & (
        position[None, None, :] < lengths_here[:, None, None]
    )
    scores = jnp.concatenate([prefix_scores, self_scores], axis=2)
    allowed = jnp.concatenate(
        [jnp.ones(prefix_scores.shape, bool), self_allowed], axis=2
    )
    row_peak = jnp.max(jnp.where(allowed, scores, -jnp.inf), axis=2, keepdims=True)
    weights = jnp.where(allowed, jnp.exp(scores - row_peak), 0.0)
    total = jnp.sum(weights, axis=2, keepdims=True)
    all_values = jnp.concatenate([prefix_values, value], axis=1)
    numerator = jnp.einsum(
        "rtk,rkd->rtd", weights.astype(jnp.bfloat16), all_values, preferred_element_type=jnp.float32
    )
    attention = (numerator / total).astype(jnp.bfloat16).reshape(row_count, HD)

    attn_terms = jnp.dot(attention, w_out, preferred_element_type=jnp.float32)
    attn_share = scatter_sum(attn_terms, "tensor", tp_count)
    middle = (state_shard.astype(jnp.float32) + attn_share).astype(jnp.bfloat16)
    middle_rows = gather_rows(middle, "tensor", tp_count)
    normed_two = rms_scale(middle_rows.astype(jnp.float32), norm_mlp)
    gate = jnp.dot(normed_two, w_gate, preferred_element_type=jnp.float32)
    upper = jnp.dot(normed_two, w_up, preferred_element_type=jnp.float32)
    hidden = (jax.nn.silu(gate) * upper).astype(jnp.bfloat16)
    down_terms = jnp.dot(hidden, w_down, preferred_element_type=jnp.float32)
    down_share = scatter_sum(down_terms, "tensor", tp_count)
    result = middle.astype(jnp.float32) + down_share
    result = (
        jnp.where(valid[:, None], result, 0.0)
        .astype(jnp.bfloat16)
        .reshape(local_reqs, L_MAX, width_here)
    )
    returned = lax.all_to_all(result, "dp", split_axis=1, concat_axis=0, tiled=True)
    hidden_out = jnp.zeros_like(returned).at[request_order].set(returned)
    return (hidden_out, keys_out, values_out)


def solution(mesh):
    in_specs = (
        P(None, "dp", "tensor"),
        P(),
        P(),
        P(),
        P(),
        P("dp", "tensor", None),
        P(),
        P(None, "tensor"),
        P(None, "tensor"),
        P(None, "tensor"),
        P("tensor", None),
        P(),
        P(None, "tensor"),
        P(None, "tensor"),
        P("tensor", None),
    )
    out_specs = (P(None, "dp", "tensor"), P("dp", None, "tensor"), P("dp", None, "tensor"))
    return jax.shard_map(shards, mesh=mesh, in_specs=in_specs, out_specs=out_specs, check_vma=False)
```

```python
import jax
import jax.numpy as jnp
import numpy as np
from jax import lax
from jax.sharding import PartitionSpec as P

H = 32
KVH = 8
HD = 64
L_MAX = 128
P_SIZE = 256


THETA = 10000000.0
EPSILON = 1e-05


def rms_scale(wide, gain):
    mean_square = jnp.mean(wide * wide, axis=-1, keepdims=True)
    return (wide * lax.rsqrt(mean_square + EPSILON) * gain.astype(jnp.float32)).astype(jnp.bfloat16)


def rotate(vectors, positions):
    half = HD // 2
    freqs = THETA ** (-(jnp.arange(half, dtype=jnp.float32) * 2.0 / HD))
    angles = positions[:, None] * freqs[None, :]
    cosine = jnp.cos(angles)
    sine = jnp.sin(angles)
    first = vectors[..., :half]
    second = vectors[..., half:]
    return jnp.concatenate(
        [first * cosine - second * sine, second * cosine + first * sine], axis=-1
    )


def gather_rows(shard, axis_name, count):
    sent = jnp.broadcast_to(shard[None], (count,) + shard.shape)
    got = lax.all_to_all(sent, axis_name, 0, 0, tiled=True)
    rows, width = shard.shape
    return got.transpose(1, 0, 2).reshape(rows, count * width)


def scatter_sum(terms, axis_name, count):
    rows, width = terms.shape
    share = width // count
    sent = terms.astype(jnp.bfloat16).reshape(rows, count, share).transpose(1, 0, 2)
    got = lax.all_to_all(sent, axis_name, 0, 0, tiled=True)
    return jnp.sum(got.astype(jnp.float32), axis=0)


def shards(
    suffix_states,
    suffix_lengths,
    request_group,
    group_owner,
    request_order,
    prefix_cache,
    norm_attn,
    w_query,
    w_key,
    w_value,
    w_out,
    norm_mlp,
    w_gate,
    w_up,
    w_down,
):
    dp_count = lax.axis_size("dp")
    tp_count = lax.axis_size("tensor")
    dp_index = lax.axis_index("dp")
    tp_index = lax.axis_index("tensor")
    total_reqs = suffix_lengths.shape[0]
    local_reqs = total_reqs // dp_count
    row_count = local_reqs * L_MAX
    heads_here = w_query.shape[1] // HD
    group_size = H // KVH
    assert heads_here == 1
    kv_cols = w_key.shape[1]
    d_here = kv_cols // KVH
    score_scale = HD ** (-0.5)
    kv_of_dest = np.arange(tp_count) * heads_here // group_size
    kv_here = tp_index * heads_here // group_size

    routed = jnp.take(suffix_states, request_order, axis=0)
    pos_here = routed.shape[1]
    width_here = routed.shape[2]
    state_part = routed.reshape(dp_count, local_reqs * pos_here * width_here)
    prefix_flat = prefix_cache.reshape(1, -1)
    prefix_part = jnp.broadcast_to(prefix_flat, (dp_count, prefix_flat.shape[1]))
    first = lax.all_to_all(
        jnp.concatenate([state_part, prefix_part], axis=1), "dp", 0, 0, tiled=True
    )
    state_split = state_part.shape[1]
    routed_here = (
        first[:, :state_split]
        .reshape(dp_count, local_reqs, pos_here, width_here)
        .transpose(1, 0, 2, 3)
        .reshape(local_reqs, dp_count * pos_here, width_here)
    )
    prefix_rows = prefix_cache.shape[1]
    prefix_all = first[:, state_split:].reshape(dp_count, prefix_rows, KVH, 2 * HD)

    state_shard = routed_here.reshape(row_count, width_here)
    slot_ids = dp_index * local_reqs + jnp.arange(local_reqs, dtype=jnp.int32)
    req_ids = jnp.take(request_order, slot_ids)
    lengths_here = jnp.take(suffix_lengths, req_ids)
    owner_here = jnp.take(group_owner, jnp.take(request_group[:, 0], req_ids))
    position = jnp.arange(L_MAX, dtype=jnp.int32)
    valid = (position[None, :] < lengths_here[:, None]).reshape(row_count)
    positions = (P_SIZE + position).astype(jnp.float32)

    chosen = jnp.take(prefix_all, owner_here, axis=0)
    chosen = jnp.take(chosen, kv_of_dest, axis=2).transpose(2, 0, 1, 3)
    picked = lax.all_to_all(chosen, "tensor", 0, 0, tiled=True)
    picked = picked.transpose(1, 0, 2, 3).reshape(local_reqs, tp_count * prefix_rows, 2 * HD)
    prefix_keys = picked[:, :, :HD]
    prefix_values = picked[:, :, HD:]

    full_rows = gather_rows(state_shard, "tensor", tp_count)
    normed = rms_scale(full_rows.astype(jnp.float32), norm_attn)
    query = jnp.dot(normed, w_query, preferred_element_type=jnp.float32).reshape(
        local_reqs, L_MAX, HD
    )
    query = rotate(query, positions).astype(jnp.bfloat16)
    kv_part = jnp.dot(
        normed, jnp.concatenate([w_key, w_value], axis=1), preferred_element_type=jnp.float32
    ).astype(jnp.bfloat16)
    pick = (np.arange(d_here)[None, :] * KVH + kv_of_dest[:, None])
    pick = np.concatenate([pick, kv_cols + pick], axis=1)
    kv_sent = jnp.take(kv_part, pick.reshape(-1), axis=1).reshape(row_count, tp_count, 2 * d_here)
    kv_got = lax.all_to_all(kv_sent.transpose(1, 0, 2), "tensor", 0, 0, tiled=True)
    key_raw = kv_got[:, :, :d_here].transpose(1, 0, 2).reshape(row_count, HD)
    value = kv_got[:, :, d_here:].transpose(1, 0, 2).reshape(row_count, HD)
    key_rot = rotate(
        key_raw.reshape(local_reqs, L_MAX, HD).astype(jnp.float32), positions
    ).astype(jnp.bfloat16)
    value = value.reshape(local_reqs, L_MAX, HD)

    valid3 = valid.reshape(local_reqs, L_MAX, 1)
    out_width = kv_cols
    out_first = (tp_index * out_width) % HD
    keys_out = jnp.where(
        valid3, lax.dynamic_slice_in_dim(key_rot, out_first, out_width, 2), 0.0
    ).astype(jnp.bfloat16)
    values_out = jnp.where(
        valid3, lax.dynamic_slice_in_dim(value, out_first, out_width, 2), 0.0
    ).astype(jnp.bfloat16)

    prefix_scores = jnp.einsum(
        "rtd,rpd->rtp", query, prefix_keys, preferred_element_type=jnp.float32
    ) * score_scale
    self_scores = jnp.einsum(
        "rtd,rsd->rts", query, key_rot, preferred_element_type=jnp.float32
    ) * score_scale
    self_allowed = (position[None, None, :] <= position[None, :, None]) & (
        position[None, None, :] < lengths_here[:, None, None]
    )
    scores = jnp.concatenate([prefix_scores, self_scores], axis=2)
    allowed = jnp.concatenate(
        [jnp.ones(prefix_scores.shape, bool), self_allowed], axis=2
    )
    row_peak = jnp.max(jnp.where(allowed, scores, -jnp.inf), axis=2, keepdims=True)
    weights = jnp.where(allowed, jnp.exp(scores - row_peak), 0.0)
    total = jnp.sum(weights, axis=2, keepdims=True)
    all_values = jnp.concatenate([prefix_values, value], axis=1)
    numerator = jnp.einsum(
        "rtk,rkd->rtd", weights.astype(jnp.bfloat16), all_values, preferred_element_type=jnp.float32
    )
    attention = (numerator / total).astype(jnp.bfloat16).reshape(row_count, HD)

    attn_terms = jnp.dot(attention, w_out, preferred_element_type=jnp.float32)
    attn_share = scatter_sum(attn_terms, "tensor", tp_count)
    middle = (state_shard.astype(jnp.float32) + attn_share).astype(jnp.bfloat16)
    middle_rows = gather_rows(middle, "tensor", tp_count)
    normed_two = rms_scale(middle_rows.astype(jnp.float32), norm_mlp)
    gate = jnp.dot(normed_two, w_gate, preferred_element_type=jnp.float32)
    upper = jnp.dot(normed_two, w_up, preferred_element_type=jnp.float32)
    hidden = (jax.nn.silu(gate) * upper).astype(jnp.bfloat16)
    down_terms = jnp.dot(hidden, w_down, preferred_element_type=jnp.float32)
    down_terms = lax.dynamic_update_slice_in_dim(
        down_terms,
        lax.dynamic_slice_in_dim(down_terms, tp_index * width_here, width_here, 1)
        + middle.astype(jnp.float32),
        tp_index * width_here,
        1,
    )
    down_terms = jnp.where(valid[:, None], down_terms, 0.0).astype(jnp.bfloat16)
    sent = down_terms.reshape(local_reqs, dp_count, pos_here, tp_count, width_here).transpose(
        1, 3, 0, 2, 4
    )
    sent = sent.reshape(dp_count * tp_count, local_reqs, pos_here, width_here)
    got = lax.all_to_all(sent, ("dp", "tensor"), 0, 0, tiled=True)
    got = got.reshape(dp_count, tp_count, local_reqs, pos_here, width_here)
    returned = (
        jnp.sum(got.astype(jnp.float32), axis=1)
        .astype(jnp.bfloat16)
        .reshape(total_reqs, pos_here, width_here)
    )
    hidden_out = jnp.zeros_like(returned).at[request_order].set(returned)
    return (hidden_out, keys_out, values_out)


def solution(mesh):
    in_specs = (
        P(None, "dp", "tensor"),
        P(),
        P(),
        P(),
        P(),
        P("dp", "tensor", None),
        P(),
        P(None, "tensor"),
        P(None, "tensor"),
        P(None, "tensor"),
        P("tensor", None),
        P(),
        P(None, "tensor"),
        P(None, "tensor"),
        P("tensor", None),
    )
    out_specs = (P(None, "dp", "tensor"), P("dp", None, "tensor"), P("dp", None, "tensor"))
    return jax.shard_map(shards, mesh=mesh, in_specs=in_specs, out_specs=out_specs, check_vma=False)
```

```python
import jax
import jax.numpy as jnp
import numpy as np
from jax import lax
from jax.sharding import PartitionSpec as P

H = 32
KVH = 8
HD = 64
L_MAX = 128
P_SIZE = 256


THETA = 10000000.0
EPSILON = 1e-05


def rms_scale(wide, gain):
    mean_square = jnp.mean(wide * wide, axis=-1, keepdims=True)
    return (wide * lax.rsqrt(mean_square + EPSILON) * gain.astype(jnp.float32)).astype(jnp.bfloat16)


def rotate(vectors, positions):
    half = HD // 2
    freqs = THETA ** (-(jnp.arange(half, dtype=jnp.float32) * 2.0 / HD))
    angles = positions[:, None] * freqs[None, :]
    cosine = jnp.cos(angles)
    sine = jnp.sin(angles)
    first = vectors[..., :half]
    second = vectors[..., half:]
    return jnp.concatenate(
        [first * cosine - second * sine, second * cosine + first * sine], axis=-1
    )


def gather_rows(shard, axis_name, count):
    sent = jnp.broadcast_to(shard[None], (count,) + shard.shape)
    got = lax.all_to_all(sent, axis_name, 0, 0, tiled=True)
    rows, width = shard.shape
    return got.transpose(1, 0, 2).reshape(rows, count * width)


def scatter_sum(terms, axis_name, count):
    rows, width = terms.shape
    share = width // count
    sent = terms.astype(jnp.bfloat16).reshape(rows, count, share).transpose(1, 0, 2)
    got = lax.all_to_all(sent, axis_name, 0, 0, tiled=True)
    return jnp.sum(got.astype(jnp.float32), axis=0)


def shards(
    suffix_states,
    suffix_lengths,
    request_group,
    group_owner,
    request_order,
    prefix_cache,
    norm_attn,
    w_query,
    w_key,
    w_value,
    w_out,
    norm_mlp,
    w_gate,
    w_up,
    w_down,
):
    dp_count = lax.axis_size("dp")
    tp_count = lax.axis_size("tensor")
    dp_index = lax.axis_index("dp")
    tp_index = lax.axis_index("tensor")
    total_reqs = suffix_lengths.shape[0]
    local_reqs = total_reqs // dp_count
    row_count = local_reqs * L_MAX
    heads_here = w_query.shape[1] // HD
    group_size = H // KVH
    assert heads_here == 1
    kv_cols = w_key.shape[1]
    d_here = kv_cols // KVH
    score_scale = HD ** (-0.5)
    kv_of_dest = np.arange(tp_count) * heads_here // group_size
    kv_here = tp_index * heads_here // group_size

    routed = jnp.take(suffix_states, request_order, axis=0)
    pos_here = routed.shape[1]
    width_here = routed.shape[2]
    state_part = routed.reshape(dp_count, local_reqs * pos_here * width_here)
    prefix_flat = prefix_cache.reshape(1, -1)
    prefix_part = jnp.broadcast_to(prefix_flat, (dp_count, prefix_flat.shape[1]))
    first = lax.all_to_all(
        jnp.concatenate([state_part, prefix_part], axis=1), "dp", 0, 0, tiled=True
    )
    state_split = state_part.shape[1]
    routed_here = (
        first[:, :state_split]
        .reshape(dp_count, local_reqs, pos_here, width_here)
        .transpose(1, 0, 2, 3)
        .reshape(local_reqs, dp_count * pos_here, width_here)
    )
    prefix_rows = prefix_cache.shape[1]
    prefix_all = first[:, state_split:].reshape(dp_count, prefix_rows, KVH, 2 * HD)

    state_shard = routed_here.reshape(row_count, width_here)
    slot_ids = dp_index * local_reqs + jnp.arange(local_reqs, dtype=jnp.int32)
    req_ids = jnp.take(request_order, slot_ids)
    lengths_here = jnp.take(suffix_lengths, req_ids)
    owner_here = jnp.take(group_owner, jnp.take(request_group[:, 0], req_ids))
    position = jnp.arange(L_MAX, dtype=jnp.int32)
    valid = (position[None, :] < lengths_here[:, None]).reshape(row_count)
    positions = (P_SIZE + position).astype(jnp.float32)

    chosen = jnp.take(prefix_all, owner_here, axis=0)
    chosen = jnp.take(chosen, kv_of_dest, axis=2).transpose(2, 0, 1, 3)
    full_rows = gather_rows(state_shard, "tensor", tp_count)
    normed = rms_scale(full_rows.astype(jnp.float32), norm_attn)
    query = jnp.dot(normed, w_query, preferred_element_type=jnp.float32).reshape(
        local_reqs, L_MAX, HD
    )
    query = rotate(query, positions).astype(jnp.bfloat16)
    kv_part = jnp.dot(
        normed, jnp.concatenate([w_key, w_value], axis=1), preferred_element_type=jnp.float32
    ).astype(jnp.bfloat16)
    pick = (np.arange(d_here)[None, :] * KVH + kv_of_dest[:, None])
    pick = np.concatenate([pick, kv_cols + pick], axis=1)
    kv_sent = jnp.take(kv_part, pick.reshape(-1), axis=1).reshape(row_count, tp_count, 2 * d_here)
    prefix_split = chosen.shape[1] * chosen.shape[2] * chosen.shape[3]
    both = lax.all_to_all(
        jnp.concatenate(
            [chosen.reshape(tp_count, -1), kv_sent.transpose(1, 0, 2).reshape(tp_count, -1)],
            axis=1,
        ),
        "tensor", 0, 0, tiled=True,
    )
    picked = both[:, :prefix_split].reshape(tp_count, local_reqs, prefix_rows, 2 * HD)
    picked = picked.transpose(1, 0, 2, 3).reshape(local_reqs, tp_count * prefix_rows, 2 * HD)
    prefix_keys = picked[:, :, :HD]
    prefix_values = picked[:, :, HD:]
    kv_got = both[:, prefix_split:].reshape(tp_count, row_count, 2 * d_here)
    key_raw = kv_got[:, :, :d_here].transpose(1, 0, 2).reshape(row_count, HD)
    value = kv_got[:, :, d_here:].transpose(1, 0, 2).reshape(row_count, HD)
    key_rot = rotate(
        key_raw.reshape(local_reqs, L_MAX, HD).astype(jnp.float32), positions
    ).astype(jnp.bfloat16)
    value = value.reshape(local_reqs, L_MAX, HD)

    valid3 = valid.reshape(local_reqs, L_MAX, 1)
    out_width = kv_cols
    out_first = (tp_index * out_width) % HD
    keys_out = jnp.where(
        valid3, lax.dynamic_slice_in_dim(key_rot, out_first, out_width, 2), 0.0
    ).astype(jnp.bfloat16)
    values_out = jnp.where(
        valid3, lax.dynamic_slice_in_dim(value, out_first, out_width, 2), 0.0
    ).astype(jnp.bfloat16)

    prefix_scores = jnp.einsum(
        "rtd,rpd->rtp", query, prefix_keys, preferred_element_type=jnp.float32
    ) * score_scale
    self_scores = jnp.einsum(
        "rtd,rsd->rts", query, key_rot, preferred_element_type=jnp.float32
    ) * score_scale
    self_allowed = (position[None, None, :] <= position[None, :, None]) & (
        position[None, None, :] < lengths_here[:, None, None]
    )
    scores = jnp.concatenate([prefix_scores, self_scores], axis=2)
    allowed = jnp.concatenate(
        [jnp.ones(prefix_scores.shape, bool), self_allowed], axis=2
    )
    row_peak = jnp.max(jnp.where(allowed, scores, -jnp.inf), axis=2, keepdims=True)
    weights = jnp.where(allowed, jnp.exp(scores - row_peak), 0.0)
    total = jnp.sum(weights, axis=2, keepdims=True)
    all_values = jnp.concatenate([prefix_values, value], axis=1)
    numerator = jnp.einsum(
        "rtk,rkd->rtd", weights.astype(jnp.bfloat16), all_values, preferred_element_type=jnp.float32
    )
    attention = (numerator / total).astype(jnp.bfloat16).reshape(row_count, HD)

    attn_terms = jnp.dot(attention, w_out, preferred_element_type=jnp.float32)
    attn_share = scatter_sum(attn_terms, "tensor", tp_count)
    middle = (state_shard.astype(jnp.float32) + attn_share).astype(jnp.bfloat16)
    middle_rows = gather_rows(middle, "tensor", tp_count)
    normed_two = rms_scale(middle_rows.astype(jnp.float32), norm_mlp)
    gate = jnp.dot(normed_two, w_gate, preferred_element_type=jnp.float32)
    upper = jnp.dot(normed_two, w_up, preferred_element_type=jnp.float32)
    hidden = (jax.nn.silu(gate) * upper).astype(jnp.bfloat16)
    down_terms = jnp.dot(hidden, w_down, preferred_element_type=jnp.float32)
    down_share = scatter_sum(down_terms, "tensor", tp_count)
    result = middle.astype(jnp.float32) + down_share
    result = (
        jnp.where(valid[:, None], result, 0.0)
        .astype(jnp.bfloat16)
        .reshape(local_reqs, L_MAX, width_here)
    )
    returned = lax.all_to_all(result, "dp", split_axis=1, concat_axis=0, tiled=True)
    hidden_out = jnp.zeros_like(returned).at[request_order].set(returned)
    return (hidden_out, keys_out, values_out)


def solution(mesh):
    in_specs = (
        P(None, "dp", "tensor"),
        P(),
        P(),
        P(),
        P(),
        P("dp", "tensor", None),
        P(),
        P(None, "tensor"),
        P(None, "tensor"),
        P(None, "tensor"),
        P("tensor", None),
        P(),
        P(None, "tensor"),
        P(None, "tensor"),
        P("tensor", None),
    )
    out_specs = (P(None, "dp", "tensor"), P("dp", None, "tensor"), P("dp", None, "tensor"))
    return jax.shard_map(shards, mesh=mesh, in_specs=in_specs, out_specs=out_specs, check_vma=False)
```

```python
import jax
import jax.numpy as jnp
import numpy as np
from jax import lax
from jax.sharding import PartitionSpec as P

H = 32
KVH = 8
HD = 64
L_MAX = 128
P_SIZE = 256


THETA = 10000000.0
EPSILON = 1e-05


def rms_scale(wide, gain):
    mean_square = jnp.mean(wide * wide, axis=-1, keepdims=True)
    return (wide * lax.rsqrt(mean_square + EPSILON) * gain.astype(jnp.float32)).astype(jnp.bfloat16)


def rotate(vectors, positions):
    half = HD // 2
    freqs = THETA ** (-(jnp.arange(half, dtype=jnp.float32) * 2.0 / HD))
    angles = positions[:, None] * freqs[None, :]
    cosine = jnp.cos(angles)
    sine = jnp.sin(angles)
    first = vectors[..., :half]
    second = vectors[..., half:]
    return jnp.concatenate(
        [first * cosine - second * sine, second * cosine + first * sine], axis=-1
    )


def gather_rows(shard, axis_name, count):
    sent = jnp.broadcast_to(shard[None], (count,) + shard.shape)
    got = lax.all_to_all(sent, axis_name, 0, 0, tiled=True)
    rows, width = shard.shape
    return got.transpose(1, 0, 2).reshape(rows, count * width)


def scatter_sum(terms, axis_name, count):
    rows, width = terms.shape
    share = width // count
    sent = terms.astype(jnp.bfloat16).reshape(rows, count, share).transpose(1, 0, 2)
    got = lax.all_to_all(sent, axis_name, 0, 0, tiled=True)
    return jnp.sum(got.astype(jnp.float32), axis=0)


def shards(
    suffix_states,
    suffix_lengths,
    request_group,
    group_owner,
    request_order,
    prefix_cache,
    norm_attn,
    w_query,
    w_key,
    w_value,
    w_out,
    norm_mlp,
    w_gate,
    w_up,
    w_down,
):
    dp_count = lax.axis_size("dp")
    tp_count = lax.axis_size("tensor")
    dp_index = lax.axis_index("dp")
    tp_index = lax.axis_index("tensor")
    total_reqs = suffix_lengths.shape[0]
    local_reqs = total_reqs // dp_count
    row_count = local_reqs * L_MAX
    heads_here = w_query.shape[1] // HD
    group_size = H // KVH
    assert heads_here == 1
    kv_cols = w_key.shape[1]
    d_here = kv_cols // KVH
    score_scale = HD ** (-0.5)
    kv_of_dest = np.arange(tp_count) * heads_here // group_size
    kv_here = tp_index * heads_here // group_size

    routed = jnp.take(suffix_states, request_order, axis=0)
    pos_here = routed.shape[1]
    width_here = routed.shape[2]
    state_part = routed.reshape(dp_count, local_reqs * pos_here * width_here)
    prefix_flat = prefix_cache.reshape(1, -1)
    prefix_part = jnp.broadcast_to(prefix_flat, (dp_count, prefix_flat.shape[1]))
    first = lax.all_to_all(
        jnp.concatenate([state_part, prefix_part], axis=1), "dp", 0, 0, tiled=True
    )
    state_split = state_part.shape[1]
    routed_here = (
        first[:, :state_split]
        .reshape(dp_count, local_reqs, pos_here, width_here)
        .transpose(1, 0, 2, 3)
        .reshape(local_reqs, dp_count * pos_here, width_here)
    )
    prefix_rows = prefix_cache.shape[1]
    prefix_all = first[:, state_split:].reshape(dp_count, prefix_rows, KVH, 2 * HD)

    state_shard = routed_here.reshape(row_count, width_here)
    slot_ids = dp_index * local_reqs + jnp.arange(local_reqs, dtype=jnp.int32)
    req_ids = jnp.take(request_order, slot_ids)
    lengths_here = jnp.take(suffix_lengths, req_ids)
    owner_here = jnp.take(group_owner, jnp.take(request_group[:, 0], req_ids))
    position = jnp.arange(L_MAX, dtype=jnp.int32)
    valid = (position[None, :] < lengths_here[:, None]).reshape(row_count)
    positions = (P_SIZE + position).astype(jnp.float32)

    chosen = jnp.take(prefix_all, owner_here, axis=0)
    chosen = jnp.take(chosen, kv_of_dest, axis=2).transpose(2, 0, 1, 3)
    full_rows = gather_rows(state_shard, "tensor", tp_count)
    normed = rms_scale(full_rows.astype(jnp.float32), norm_attn)
    query = jnp.dot(normed, w_query, preferred_element_type=jnp.float32).reshape(
        local_reqs, L_MAX, HD
    )
    query = rotate(query, positions).astype(jnp.bfloat16)
    kv_part = jnp.dot(
        normed, jnp.concatenate([w_key, w_value], axis=1), preferred_element_type=jnp.float32
    ).astype(jnp.bfloat16)
    pick = (np.arange(d_here)[None, :] * KVH + kv_of_dest[:, None])
    pick = np.concatenate([pick, kv_cols + pick], axis=1)
    kv_sent = jnp.take(kv_part, pick.reshape(-1), axis=1).reshape(row_count, tp_count, 2 * d_here)
    prefix_split = chosen.shape[1] * chosen.shape[2] * chosen.shape[3]
    both = lax.all_to_all(
        jnp.concatenate(
            [chosen.reshape(tp_count, -1), kv_sent.transpose(1, 0, 2).reshape(tp_count, -1)],
            axis=1,
        ),
        "tensor", 0, 0, tiled=True,
    )
    picked = both[:, :prefix_split].reshape(tp_count, local_reqs, prefix_rows, 2 * HD)
    picked = picked.transpose(1, 0, 2, 3).reshape(local_reqs, tp_count * prefix_rows, 2 * HD)
    prefix_keys = picked[:, :, :HD]
    prefix_values = picked[:, :, HD:]
    kv_got = both[:, prefix_split:].reshape(tp_count, row_count, 2 * d_here)
    key_raw = kv_got[:, :, :d_here].transpose(1, 0, 2).reshape(row_count, HD)
    value = kv_got[:, :, d_here:].transpose(1, 0, 2).reshape(row_count, HD)
    key_rot = rotate(
        key_raw.reshape(local_reqs, L_MAX, HD).astype(jnp.float32), positions
    ).astype(jnp.bfloat16)
    value = value.reshape(local_reqs, L_MAX, HD)

    valid3 = valid.reshape(local_reqs, L_MAX, 1)
    out_width = kv_cols
    out_first = (tp_index * out_width) % HD
    keys_out = jnp.where(
        valid3, lax.dynamic_slice_in_dim(key_rot, out_first, out_width, 2), 0.0
    ).astype(jnp.bfloat16)
    values_out = jnp.where(
        valid3, lax.dynamic_slice_in_dim(value, out_first, out_width, 2), 0.0
    ).astype(jnp.bfloat16)

    prefix_scores = jnp.einsum(
        "rtd,rpd->rtp", query, prefix_keys, preferred_element_type=jnp.float32
    ) * score_scale
    self_scores = jnp.einsum(
        "rtd,rsd->rts", query, key_rot, preferred_element_type=jnp.float32
    ) * score_scale
    self_allowed = (position[None, None, :] <= position[None, :, None]) & (
        position[None, None, :] < lengths_here[:, None, None]
    )
    scores = jnp.concatenate([prefix_scores, self_scores], axis=2)
    allowed = jnp.concatenate(
        [jnp.ones(prefix_scores.shape, bool), self_allowed], axis=2
    )
    row_peak = jnp.max(jnp.where(allowed, scores, -jnp.inf), axis=2, keepdims=True)
    weights = jnp.where(allowed, jnp.exp(scores - row_peak), 0.0)
    total = jnp.sum(weights, axis=2, keepdims=True)
    all_values = jnp.concatenate([prefix_values, value], axis=1)
    numerator = jnp.einsum(
        "rtk,rkd->rtd", weights.astype(jnp.bfloat16), all_values, preferred_element_type=jnp.float32
    )
    attention = (numerator / total).astype(jnp.bfloat16).reshape(row_count, HD)

    attn_terms = jnp.dot(attention, w_out, preferred_element_type=jnp.float32)
    attn_share = scatter_sum(attn_terms, "tensor", tp_count)
    middle = (state_shard.astype(jnp.float32) + attn_share).astype(jnp.bfloat16)
    middle_rows = gather_rows(middle, "tensor", tp_count)
    normed_two = rms_scale(middle_rows.astype(jnp.float32), norm_mlp)
    gate = jnp.dot(normed_two, w_gate, preferred_element_type=jnp.float32)
    upper = jnp.dot(normed_two, w_up, preferred_element_type=jnp.float32)
    hidden = (jax.nn.silu(gate) * upper).astype(jnp.bfloat16)
    pos_blocks = L_MAX // pos_here
    row_perm = (
        np.arange(row_count).reshape(local_reqs, pos_blocks, pos_here).transpose(1, 0, 2).reshape(-1)
    )
    hidden_perm = jnp.take(hidden, row_perm, axis=0)
    down_terms = jnp.dot(hidden_perm, w_down, preferred_element_type=jnp.float32)
    down_terms = down_terms.reshape(row_count, tp_count, width_here)
    own = (jnp.arange(tp_count) == tp_index)[None, :, None]
    middle_perm = jnp.take(middle, row_perm, axis=0).astype(jnp.float32)[:, None, :]
    valid_perm = jnp.take(valid, row_perm)[:, None, None]
    sent = jnp.where(valid_perm, down_terms + jnp.where(own, middle_perm, 0.0), 0.0)
    sent = sent.astype(jnp.bfloat16).reshape(pos_blocks, local_reqs * pos_here, tp_count, width_here)
    sent = sent.transpose(0, 2, 1, 3).reshape(pos_blocks * tp_count, local_reqs * pos_here, width_here)
    got = lax.all_to_all(sent, ("dp", "tensor"), 0, 0, tiled=True)
    got = got.reshape(dp_count, tp_count, local_reqs * pos_here, width_here)
    returned = (
        jnp.sum(got.astype(jnp.float32), axis=1)
        .astype(jnp.bfloat16)
        .reshape(total_reqs, pos_here, width_here)
    )
    hidden_out = jnp.zeros_like(returned).at[request_order].set(returned)
    return (hidden_out, keys_out, values_out)


def solution(mesh):
    in_specs = (
        P(None, "dp", "tensor"),
        P(),
        P(),
        P(),
        P(),
        P("dp", "tensor", None),
        P(),
        P(None, "tensor"),
        P(None, "tensor"),
        P(None, "tensor"),
        P("tensor", None),
        P(),
        P(None, "tensor"),
        P(None, "tensor"),
        P("tensor", None),
    )
    out_specs = (P(None, "dp", "tensor"), P("dp", None, "tensor"), P("dp", None, "tensor"))
    return jax.shard_map(shards, mesh=mesh, in_specs=in_specs, out_specs=out_specs, check_vma=False)
```

```python
import jax
import jax.numpy as jnp
import numpy as np
from jax import lax
from jax.sharding import PartitionSpec as P

H = 32
KVH = 8
HD = 64
L_MAX = 128
P_SIZE = 256


THETA = 10000000.0
EPSILON = 1e-05


def rms_scale(wide, gain):
    mean_square = jnp.mean(wide * wide, axis=-1, keepdims=True)
    return (wide * lax.rsqrt(mean_square + EPSILON) * gain.astype(jnp.float32)).astype(jnp.bfloat16)


def rotate(vectors, positions):
    half = HD // 2
    freqs = THETA ** (-(jnp.arange(half, dtype=jnp.float32) * 2.0 / HD))
    angles = positions[:, None] * freqs[None, :]
    cosine = jnp.cos(angles)
    sine = jnp.sin(angles)
    first = vectors[..., :half]
    second = vectors[..., half:]
    return jnp.concatenate(
        [first * cosine - second * sine, second * cosine + first * sine], axis=-1
    )


def gather_rows(shard, axis_name, count):
    sent = jnp.broadcast_to(shard[None], (count,) + shard.shape)
    got = lax.all_to_all(sent, axis_name, 0, 0, tiled=True)
    rows, width = shard.shape
    return got.transpose(1, 0, 2).reshape(rows, count * width)


def scatter_sum(terms, axis_name, count):
    rows, width = terms.shape
    share = width // count
    sent = terms.astype(jnp.bfloat16).reshape(rows, count, share).transpose(1, 0, 2)
    got = lax.all_to_all(sent, axis_name, 0, 0, tiled=True)
    return jnp.sum(got.astype(jnp.float32), axis=0)


def shards(
    suffix_states,
    suffix_lengths,
    request_group,
    group_owner,
    request_order,
    prefix_cache,
    norm_attn,
    w_query,
    w_key,
    w_value,
    w_out,
    norm_mlp,
    w_gate,
    w_up,
    w_down,
):
    dp_count = lax.axis_size("dp")
    tp_count = lax.axis_size("tensor")
    dp_index = lax.axis_index("dp")
    tp_index = lax.axis_index("tensor")
    total_reqs = suffix_lengths.shape[0]
    local_reqs = total_reqs // dp_count
    row_count = local_reqs * L_MAX
    heads_here = w_query.shape[1] // HD
    group_size = H // KVH
    assert heads_here == 1
    kv_cols = w_key.shape[1]
    d_here = kv_cols // KVH
    score_scale = HD ** (-0.5)
    kv_of_dest = np.arange(tp_count) * heads_here // group_size
    kv_here = tp_index * heads_here // group_size

    routed = jnp.take(suffix_states, request_order, axis=0)
    pos_here = routed.shape[1]
    width_here = routed.shape[2]
    state_part = routed.reshape(dp_count, local_reqs * pos_here * width_here)
    first = lax.all_to_all(state_part, "dp", 0, 0, tiled=True)
    shifted = [prefix_cache[0]] + [
        lax.ppermute(prefix_cache[0], "dp", [(i, (i + k) % dp_count) for i in range(dp_count)])
        for k in range(1, dp_count)
    ]
    prefix_stack = jnp.stack(shifted)
    routed_here = (
        first
        .reshape(dp_count, local_reqs, pos_here, width_here)
        .transpose(1, 0, 2, 3)
        .reshape(local_reqs, dp_count * pos_here, width_here)
    )
    prefix_rows = prefix_cache.shape[1]
    prefix_all = prefix_stack.reshape(dp_count, prefix_rows, KVH, 2 * HD)

    state_shard = routed_here.reshape(row_count, width_here)
    slot_ids = dp_index * local_reqs + jnp.arange(local_reqs, dtype=jnp.int32)
    req_ids = jnp.take(request_order, slot_ids)
    lengths_here = jnp.take(suffix_lengths, req_ids)
    owner_here = jnp.take(group_owner, jnp.take(request_group[:, 0], req_ids))
    position = jnp.arange(L_MAX, dtype=jnp.int32)
    valid = (position[None, :] < lengths_here[:, None]).reshape(row_count)
    positions = (P_SIZE + position).astype(jnp.float32)

    chosen = jnp.take(prefix_all, (dp_index - owner_here) % dp_count, axis=0)
    chosen = jnp.take(chosen, kv_of_dest, axis=2).transpose(2, 0, 1, 3)
    full_rows = gather_rows(state_shard, "tensor", tp_count)
    normed = rms_scale(full_rows.astype(jnp.float32), norm_attn)
    query = jnp.dot(normed, w_query, preferred_element_type=jnp.float32).reshape(
        local_reqs, L_MAX, HD
    )
    query = rotate(query, positions).astype(jnp.bfloat16)
    kv_part = jnp.dot(
        normed, jnp.concatenate([w_key, w_value], axis=1), preferred_element_type=jnp.float32
    ).astype(jnp.bfloat16)
    pick = (np.arange(d_here)[None, :] * KVH + kv_of_dest[:, None])
    pick = np.concatenate([pick, kv_cols + pick], axis=1)
    kv_sent = jnp.take(kv_part, pick.reshape(-1), axis=1).reshape(row_count, tp_count, 2 * d_here)
    prefix_split = chosen.shape[1] * chosen.shape[2] * chosen.shape[3]
    both = lax.all_to_all(
        jnp.concatenate(
            [chosen.reshape(tp_count, -1), kv_sent.transpose(1, 0, 2).reshape(tp_count, -1)],
            axis=1,
        ),
        "tensor", 0, 0, tiled=True,
    )
    picked = both[:, :prefix_split].reshape(tp_count, local_reqs, prefix_rows, 2 * HD)
    picked = picked.transpose(1, 0, 2, 3).reshape(local_reqs, tp_count * prefix_rows, 2 * HD)
    prefix_keys = picked[:, :, :HD]
    prefix_values = picked[:, :, HD:]
    kv_got = both[:, prefix_split:].reshape(tp_count, row_count, 2 * d_here)
    key_raw = kv_got[:, :, :d_here].transpose(1, 0, 2).reshape(row_count, HD)
    value = kv_got[:, :, d_here:].transpose(1, 0, 2).reshape(row_count, HD)
    key_rot = rotate(
        key_raw.reshape(local_reqs, L_MAX, HD).astype(jnp.float32), positions
    ).astype(jnp.bfloat16)
    value = value.reshape(local_reqs, L_MAX, HD)

    valid3 = valid.reshape(local_reqs, L_MAX, 1)
    out_width = kv_cols
    out_first = (tp_index * out_width) % HD
    keys_out = jnp.where(
        valid3, lax.dynamic_slice_in_dim(key_rot, out_first, out_width, 2), 0.0
    ).astype(jnp.bfloat16)
    values_out = jnp.where(
        valid3, lax.dynamic_slice_in_dim(value, out_first, out_width, 2), 0.0
    ).astype(jnp.bfloat16)

    prefix_scores = jnp.einsum(
        "rtd,rpd->rtp", query, prefix_keys, preferred_element_type=jnp.float32
    ) * score_scale
    self_scores = jnp.einsum(
        "rtd,rsd->rts", query, key_rot, preferred_element_type=jnp.float32
    ) * score_scale
    self_allowed = (position[None, None, :] <= position[None, :, None]) & (
        position[None, None, :] < lengths_here[:, None, None]
    )
    scores = jnp.concatenate([prefix_scores, self_scores], axis=2)
    allowed = jnp.concatenate(
        [jnp.ones(prefix_scores.shape, bool), self_allowed], axis=2
    )
    row_peak = jnp.max(jnp.where(allowed, scores, -jnp.inf), axis=2, keepdims=True)
    weights = jnp.where(allowed, jnp.exp(scores - row_peak), 0.0)
    total = jnp.sum(weights, axis=2, keepdims=True)
    all_values = jnp.concatenate([prefix_values, value], axis=1)
    numerator = jnp.einsum(
        "rtk,rkd->rtd", weights.astype(jnp.bfloat16), all_values, preferred_element_type=jnp.float32
    )
    attention = (numerator / total).astype(jnp.bfloat16).reshape(row_count, HD)

    attn_terms = jnp.dot(attention, w_out, preferred_element_type=jnp.float32)
    attn_share = scatter_sum(attn_terms, "tensor", tp_count)
    middle = (state_shard.astype(jnp.float32) + attn_share).astype(jnp.bfloat16)
    middle_rows = gather_rows(middle, "tensor", tp_count)
    normed_two = rms_scale(middle_rows.astype(jnp.float32), norm_mlp)
    gate = jnp.dot(normed_two, w_gate, preferred_element_type=jnp.float32)
    upper = jnp.dot(normed_two, w_up, preferred_element_type=jnp.float32)
    hidden = (jax.nn.silu(gate) * upper).astype(jnp.bfloat16)
    down_terms = jnp.dot(hidden, w_down, preferred_element_type=jnp.float32)
    down_share = scatter_sum(down_terms, "tensor", tp_count)
    result = middle.astype(jnp.float32) + down_share
    result = (
        jnp.where(valid[:, None], result, 0.0)
        .astype(jnp.bfloat16)
        .reshape(local_reqs, L_MAX, width_here)
    )
    returned = lax.all_to_all(result, "dp", split_axis=1, concat_axis=0, tiled=True)
    hidden_out = jnp.zeros_like(returned).at[request_order].set(returned)
    return (hidden_out, keys_out, values_out)


def solution(mesh):
    in_specs = (
        P(None, "dp", "tensor"),
        P(),
        P(),
        P(),
        P(),
        P("dp", "tensor", None),
        P(),
        P(None, "tensor"),
        P(None, "tensor"),
        P(None, "tensor"),
        P("tensor", None),
        P(),
        P(None, "tensor"),
        P(None, "tensor"),
        P("tensor", None),
    )
    out_specs = (P(None, "dp", "tensor"), P("dp", None, "tensor"), P("dp", None, "tensor"))
    return jax.shard_map(shards, mesh=mesh, in_specs=in_specs, out_specs=out_specs, check_vma=False)
```

```python
import jax
import jax.numpy as jnp
import numpy as np
from jax import lax
from jax.sharding import PartitionSpec as P

H = 32
KVH = 8
HD = 64
L_MAX = 128
P_SIZE = 256


THETA = 10000000.0
EPSILON = 1e-05


def rms_scale(wide, gain):
    mean_square = jnp.mean(wide * wide, axis=-1, keepdims=True)
    return (wide * lax.rsqrt(mean_square + EPSILON) * gain.astype(jnp.float32)).astype(jnp.bfloat16)


def rotate(vectors, positions):
    half = HD // 2
    freqs = THETA ** (-(jnp.arange(half, dtype=jnp.float32) * 2.0 / HD))
    angles = positions[:, None] * freqs[None, :]
    cosine = jnp.cos(angles)
    sine = jnp.sin(angles)
    first = vectors[..., :half]
    second = vectors[..., half:]
    return jnp.concatenate(
        [first * cosine - second * sine, second * cosine + first * sine], axis=-1
    )


def gather_rows(shard, axis_name, count):
    sent = jnp.broadcast_to(shard[None], (count,) + shard.shape)
    got = lax.all_to_all(sent, axis_name, 0, 0, tiled=True)
    rows, width = shard.shape
    return got.transpose(1, 0, 2).reshape(rows, count * width)


def scatter_sum(terms, axis_name, count):
    rows, width = terms.shape
    share = width // count
    sent = terms.astype(jnp.bfloat16).reshape(rows, count, share).transpose(1, 0, 2)
    got = lax.all_to_all(sent, axis_name, 0, 0, tiled=True)
    return jnp.sum(got.astype(jnp.float32), axis=0)


def shards(
    suffix_states,
    suffix_lengths,
    request_group,
    group_owner,
    request_order,
    prefix_cache,
    norm_attn,
    w_query,
    w_key,
    w_value,
    w_out,
    norm_mlp,
    w_gate,
    w_up,
    w_down,
):
    dp_count = lax.axis_size("dp")
    tp_count = lax.axis_size("tensor")
    dp_index = lax.axis_index("dp")
    tp_index = lax.axis_index("tensor")
    total_reqs = suffix_lengths.shape[0]
    local_reqs = total_reqs // dp_count
    row_count = local_reqs * L_MAX
    heads_here = w_query.shape[1] // HD
    group_size = H // KVH
    assert heads_here == 1 and local_reqs == 2
    kv_cols = w_key.shape[1]
    d_here = kv_cols // KVH
    score_scale = HD ** (-0.5)
    kv_of_dest = np.arange(tp_count) * heads_here // group_size
    kv_here = tp_index * heads_here // group_size

    routed = jnp.take(suffix_states, request_order, axis=0)
    pos_here = routed.shape[1]
    width_here = routed.shape[2]
    state_part = routed.reshape(dp_count, local_reqs * pos_here * width_here)
    prefix_flat = prefix_cache.reshape(1, -1)
    prefix_part = jnp.broadcast_to(prefix_flat, (dp_count, prefix_flat.shape[1]))
    first = lax.all_to_all(
        jnp.concatenate([state_part, prefix_part], axis=1), "dp", 0, 0, tiled=True
    )
    state_split = state_part.shape[1]
    routed_here = (
        first[:, :state_split]
        .reshape(dp_count, local_reqs, pos_here, width_here)
        .transpose(1, 0, 2, 3)
        .reshape(local_reqs, dp_count * pos_here, width_here)
    )
    prefix_rows = prefix_cache.shape[1]
    prefix_all = first[:, state_split:].reshape(dp_count, prefix_rows, KVH, 2 * HD)

    state_shard = routed_here.reshape(row_count, width_here)
    slot_ids = dp_index * local_reqs + jnp.arange(local_reqs, dtype=jnp.int32)
    req_ids = jnp.take(request_order, slot_ids)
    lengths_here = jnp.take(suffix_lengths, req_ids)
    owner_here = jnp.take(group_owner, jnp.take(request_group[:, 0], req_ids))
    position = jnp.arange(L_MAX, dtype=jnp.int32)
    valid = (position[None, :] < lengths_here[:, None]).reshape(row_count)
    positions = (P_SIZE + position).astype(jnp.float32)

    chosen = jnp.take(prefix_all, owner_here, axis=0)
    chosen = jnp.take(chosen, kv_of_dest, axis=2).transpose(2, 0, 1, 3)
    full_rows = gather_rows(state_shard, "tensor", tp_count)
    normed = rms_scale(full_rows.astype(jnp.float32), norm_attn)
    query = jnp.dot(normed, w_query, preferred_element_type=jnp.float32).reshape(
        local_reqs, L_MAX, HD
    )
    query = rotate(query, positions).astype(jnp.bfloat16)
    kv_part = jnp.dot(
        normed, jnp.concatenate([w_key, w_value], axis=1), preferred_element_type=jnp.float32
    ).astype(jnp.bfloat16)
    pick = (np.arange(d_here)[None, :] * KVH + kv_of_dest[:, None])
    pick = np.concatenate([pick, kv_cols + pick], axis=1)
    kv_sent = jnp.take(kv_part, pick.reshape(-1), axis=1).reshape(row_count, tp_count, 2 * d_here)
    prefix_split = chosen.shape[1] * chosen.shape[2] * chosen.shape[3]
    both = lax.all_to_all(
        jnp.concatenate(
            [chosen.reshape(tp_count, -1), kv_sent.transpose(1, 0, 2).reshape(tp_count, -1)],
            axis=1,
        ),
        "tensor", 0, 0, tiled=True,
    )
    picked = both[:, :prefix_split].reshape(tp_count, local_reqs, prefix_rows, 2 * HD)
    picked = picked.transpose(1, 0, 2, 3).reshape(local_reqs, tp_count * prefix_rows, 2 * HD)
    prefix_keys = picked[:, :, :HD]
    prefix_values = picked[:, :, HD:]
    kv_got = both[:, prefix_split:].reshape(tp_count, row_count, 2 * d_here)
    key_raw = kv_got[:, :, :d_here].transpose(1, 0, 2).reshape(row_count, HD)
    value = kv_got[:, :, d_here:].transpose(1, 0, 2).reshape(row_count, HD)
    key_rot = rotate(
        key_raw.reshape(local_reqs, L_MAX, HD).astype(jnp.float32), positions
    ).astype(jnp.bfloat16)
    value = value.reshape(local_reqs, L_MAX, HD)

    valid3 = valid.reshape(local_reqs, L_MAX, 1)
    out_width = kv_cols
    out_first = (tp_index * out_width) % HD
    keys_out = jnp.where(
        valid3, lax.dynamic_slice_in_dim(key_rot, out_first, out_width, 2), 0.0
    ).astype(jnp.bfloat16)
    values_out = jnp.where(
        valid3, lax.dynamic_slice_in_dim(value, out_first, out_width, 2), 0.0
    ).astype(jnp.bfloat16)

    prefix_scores = jnp.einsum(
        "rtd,rpd->rtp", query, prefix_keys, preferred_element_type=jnp.float32
    ) * score_scale
    self_scores = jnp.einsum(
        "rtd,rsd->rts", query, key_rot, preferred_element_type=jnp.float32
    ) * score_scale
    self_allowed = (position[None, None, :] <= position[None, :, None]) & (
        position[None, None, :] < lengths_here[:, None, None]
    )
    scores = jnp.concatenate([prefix_scores, self_scores], axis=2)
    allowed = jnp.concatenate(
        [jnp.ones(prefix_scores.shape, bool), self_allowed], axis=2
    )
    row_peak = jnp.max(jnp.where(allowed, scores, -jnp.inf), axis=2, keepdims=True)
    weights = jnp.where(allowed, jnp.exp(scores - row_peak), 0.0)
    total = jnp.sum(weights, axis=2, keepdims=True)
    all_values = jnp.concatenate([prefix_values, value], axis=1)
    numerator = jnp.einsum(
        "rtk,rkd->rtd", weights.astype(jnp.bfloat16), all_values, preferred_element_type=jnp.float32
    )
    attention = (numerator / total).astype(jnp.bfloat16).reshape(row_count, HD)

    attn_terms = jnp.dot(attention, w_out, preferred_element_type=jnp.float32)
    attn_share = scatter_sum(attn_terms, "tensor", tp_count)
    middle = (state_shard.astype(jnp.float32) + attn_share).astype(jnp.bfloat16)
    core = tp_index % 2
    pair = [(t, t ^ 1) for t in range(tp_count)]
    w_gu_sib, w_down_sib = lax.ppermute(
        (jnp.concatenate([w_gate, w_up], axis=1), w_down), "tensor", pair
    )
    units = w_gate.shape[1]
    w_gate_chip = jnp.concatenate([w_gate, w_gu_sib[:, :units]], axis=1)
    w_up_chip = jnp.concatenate([w_up, w_gu_sib[:, units:]], axis=1)
    w_down_chip = jnp.concatenate([w_down, w_down_sib], axis=0)
    middle_req = middle.reshape(local_reqs, L_MAX, width_here)
    sent = jnp.take(middle_req, np.arange(tp_count) % 2, axis=0)
    got = lax.all_to_all(sent, "tensor", 0, 0, tiled=True)
    middle_rows = got.transpose(1, 0, 2).reshape(L_MAX, tp_count * width_here)
    normed_two = rms_scale(middle_rows.astype(jnp.float32), norm_mlp)
    gate = jnp.dot(normed_two, w_gate_chip, preferred_element_type=jnp.float32)
    upper = jnp.dot(normed_two, w_up_chip, preferred_element_type=jnp.float32)
    hidden = (jax.nn.silu(gate) * upper).astype(jnp.bfloat16)
    down_terms = jnp.dot(hidden, w_down_chip, preferred_element_type=jnp.float32)
    sent = down_terms.astype(jnp.bfloat16).reshape(L_MAX, tp_count, width_here).transpose(1, 0, 2)
    got = lax.all_to_all(sent, "tensor", 0, 0, tiled=True)
    down_share = jnp.sum(
        got.reshape(tp_count // 2, local_reqs, L_MAX, width_here).astype(jnp.float32), axis=0
    ).reshape(row_count, width_here)
    result = middle.astype(jnp.float32) + down_share
    result = (
        jnp.where(valid[:, None], result, 0.0)
        .astype(jnp.bfloat16)
        .reshape(local_reqs, L_MAX, width_here)
    )
    returned = lax.all_to_all(result, "dp", split_axis=1, concat_axis=0, tiled=True)
    hidden_out = jnp.zeros_like(returned).at[request_order].set(returned)
    return (hidden_out, keys_out, values_out)


def solution(mesh):
    in_specs = (
        P(None, "dp", "tensor"),
        P(),
        P(),
        P(),
        P(),
        P("dp", "tensor", None),
        P(),
        P(None, "tensor"),
        P(None, "tensor"),
        P(None, "tensor"),
        P("tensor", None),
        P(),
        P(None, "tensor"),
        P(None, "tensor"),
        P("tensor", None),
    )
    out_specs = (P(None, "dp", "tensor"), P("dp", None, "tensor"), P("dp", None, "tensor"))
    return jax.shard_map(shards, mesh=mesh, in_specs=in_specs, out_specs=out_specs, check_vma=False)
```

```python
import jax
import jax.numpy as jnp
import numpy as np
from jax import lax
from jax.sharding import PartitionSpec as P

H = 32
KVH = 8
HD = 64
L_MAX = 128
P_SIZE = 256


THETA = 10000000.0
EPSILON = 1e-05


def rms_scale(wide, gain):
    mean_square = jnp.mean(wide * wide, axis=-1, keepdims=True)
    return (wide * lax.rsqrt(mean_square + EPSILON) * gain.astype(jnp.float32)).astype(jnp.bfloat16)


def rotate(vectors, positions):
    half = HD // 2
    freqs = THETA ** (-(jnp.arange(half, dtype=jnp.float32) * 2.0 / HD))
    angles = positions[:, None] * freqs[None, :]
    cosine = jnp.cos(angles)
    sine = jnp.sin(angles)
    first = vectors[..., :half]
    second = vectors[..., half:]
    return jnp.concatenate(
        [first * cosine - second * sine, second * cosine + first * sine], axis=-1
    )


def gather_rows(shard, axis_name, count):
    sent = jnp.broadcast_to(shard[None], (count,) + shard.shape)
    got = lax.all_to_all(sent, axis_name, 0, 0, tiled=True)
    rows, width = shard.shape
    return got.transpose(1, 0, 2).reshape(rows, count * width)


def scatter_sum(terms, axis_name, count):
    rows, width = terms.shape
    share = width // count
    sent = terms.astype(jnp.bfloat16).reshape(rows, count, share).transpose(1, 0, 2)
    got = lax.all_to_all(sent, axis_name, 0, 0, tiled=True)
    return jnp.sum(got.astype(jnp.float32), axis=0)


def shards(
    suffix_states,
    suffix_lengths,
    request_group,
    group_owner,
    request_order,
    prefix_cache,
    norm_attn,
    w_query,
    w_key,
    w_value,
    w_out,
    norm_mlp,
    w_gate,
    w_up,
    w_down,
):
    dp_count = lax.axis_size("dp")
    tp_count = lax.axis_size("tensor")
    dp_index = lax.axis_index("dp")
    tp_index = lax.axis_index("tensor")
    total_reqs = suffix_lengths.shape[0]
    local_reqs = total_reqs // dp_count
    row_count = local_reqs * L_MAX
    heads_here = w_query.shape[1] // HD
    group_size = H // KVH
    assert heads_here == 1 and local_reqs == 2
    kv_cols = w_key.shape[1]
    d_here = kv_cols // KVH
    score_scale = HD ** (-0.5)
    kv_of_dest = np.arange(tp_count) * heads_here // group_size
    kv_here = tp_index * heads_here // group_size

    routed = jnp.take(suffix_states, request_order, axis=0)
    pos_here = routed.shape[1]
    width_here = routed.shape[2]
    state_part = routed.reshape(dp_count, local_reqs * pos_here * width_here)
    prefix_flat = prefix_cache.reshape(1, -1)
    prefix_part = jnp.broadcast_to(prefix_flat, (dp_count, prefix_flat.shape[1]))
    first = lax.all_to_all(
        jnp.concatenate([state_part, prefix_part], axis=1), "dp", 0, 0, tiled=True
    )
    state_split = state_part.shape[1]
    routed_here = (
        first[:, :state_split]
        .reshape(dp_count, local_reqs, pos_here, width_here)
        .transpose(1, 0, 2, 3)
        .reshape(local_reqs, dp_count * pos_here, width_here)
    )
    prefix_rows = prefix_cache.shape[1]
    prefix_all = first[:, state_split:].reshape(dp_count, prefix_rows, KVH, 2 * HD)

    state_shard = routed_here.reshape(row_count, width_here)
    slot_ids = dp_index * local_reqs + jnp.arange(local_reqs, dtype=jnp.int32)
    req_ids = jnp.take(request_order, slot_ids)
    lengths_here = jnp.take(suffix_lengths, req_ids)
    owner_here = jnp.take(group_owner, jnp.take(request_group[:, 0], req_ids))
    position = jnp.arange(L_MAX, dtype=jnp.int32)
    valid = (position[None, :] < lengths_here[:, None]).reshape(row_count)
    positions = (P_SIZE + position).astype(jnp.float32)

    core = tp_index % 2
    pair = [(t, t ^ 1) for t in range(tp_count)]
    q_cols = w_query.shape[1]
    w_qkv_sib = lax.ppermute(jnp.concatenate([w_query, w_key, w_value], axis=1), "tensor", pair)
    w_query_chip = jnp.concatenate([w_query, w_qkv_sib[:, :q_cols]], axis=1)
    w_key_chip = jnp.concatenate([w_key, w_qkv_sib[:, q_cols : q_cols + kv_cols]], axis=1)
    w_value_chip = jnp.concatenate([w_value, w_qkv_sib[:, q_cols + kv_cols :]], axis=1)

    chosen = jnp.take(prefix_all, jnp.take(owner_here, np.arange(tp_count) % 2), axis=0)
    chosen = jnp.take_along_axis(
        chosen, jnp.asarray(kv_of_dest).reshape(tp_count, 1, 1, 1), axis=2
    ).reshape(tp_count, prefix_rows, 2 * HD)

    state_req = routed_here
    sent = jnp.take(state_req, np.arange(tp_count) % 2, axis=0)
    got = lax.all_to_all(sent, "tensor", 0, 0, tiled=True)
    full_rows = got.transpose(1, 0, 2).reshape(L_MAX, tp_count * width_here)
    normed = rms_scale(full_rows.astype(jnp.float32), norm_attn)
    query = jnp.dot(normed, w_query_chip, preferred_element_type=jnp.float32)
    query = query.reshape(L_MAX, 2 * heads_here, HD).transpose(1, 0, 2)
    query = rotate(query, positions).astype(jnp.bfloat16)
    kv_part = jnp.dot(
        normed, jnp.concatenate([w_key_chip, w_value_chip], axis=1), preferred_element_type=jnp.float32
    ).astype(jnp.bfloat16)
    chip_d = 2 * d_here
    pick = (np.arange(d_here)[None, :] * KVH + kv_of_dest[:, None])
    pick = np.concatenate(
        [pick, kv_cols + pick, 2 * kv_cols + pick, 3 * kv_cols + pick], axis=1
    )
    kv_all = jnp.concatenate(
        [kv_part[:, :kv_cols], kv_part[:, kv_cols : 2 * kv_cols],
         kv_part[:, 2 * kv_cols : 3 * kv_cols], kv_part[:, 3 * kv_cols :]], axis=1
    )
    kv_sent = jnp.take(kv_all, pick.reshape(-1), axis=1).reshape(L_MAX, tp_count, 2 * chip_d)
    prefix_split = chosen.shape[1] * chosen.shape[2]
    both = lax.all_to_all(
        jnp.concatenate(
            [chosen.reshape(tp_count, -1), kv_sent.transpose(1, 0, 2).reshape(tp_count, -1)],
            axis=1,
        ),
        "tensor", 0, 0, tiled=True,
    )
    picked = both[:, :prefix_split].reshape(tp_count, prefix_rows, 2 * HD)
    picked = picked.reshape(tp_count * prefix_rows, 2 * HD)
    prefix_keys = picked[:, :HD]
    prefix_values = picked[:, HD:]
    kv_got = both[:, prefix_split:].reshape(tp_count // 2, 2, L_MAX, 2 * chip_d)
    kv_got = jnp.take(kv_got, core, axis=1)
    src_t = (np.arange(tp_count // 2) * 2)[:, None]
    keys4 = kv_got[:, :, : 2 * d_here].reshape(tp_count // 2, L_MAX, 2, d_here)
    vals4 = kv_got[:, :, 2 * d_here :].reshape(tp_count // 2, L_MAX, 2, d_here)
    flip = core == 1
    keys4 = jnp.where(flip, keys4[:, :, ::-1], keys4)
    vals4 = jnp.where(flip, vals4[:, :, ::-1], vals4)
    key_raw = keys4.transpose(1, 0, 2, 3).reshape(L_MAX, HD)
    value = vals4.transpose(1, 0, 2, 3).reshape(L_MAX, HD)
    key_rot = rotate(key_raw.astype(jnp.float32), positions).astype(jnp.bfloat16)

    out_width = kv_cols
    out_first = (tp_index * out_width) % HD
    sib_first = ((tp_index ^ 1) * out_width) % HD
    kv_for_sib = jnp.concatenate(
        [lax.dynamic_slice_in_dim(key_rot, sib_first, out_width, 1),
         lax.dynamic_slice_in_dim(value, sib_first, out_width, 1)], axis=1
    )
    kv_from_sib = lax.ppermute(kv_for_sib, "tensor", pair)
    kv_mine = jnp.concatenate(
        [lax.dynamic_slice_in_dim(key_rot, out_first, out_width, 1),
         lax.dynamic_slice_in_dim(value, out_first, out_width, 1)], axis=1
    )
    kv_two = jnp.where(
        core == 0, jnp.stack([kv_mine, kv_from_sib]), jnp.stack([kv_from_sib, kv_mine])
    )
    valid3 = valid.reshape(local_reqs, L_MAX, 1)
    keys_out = jnp.where(valid3, kv_two[:, :, :out_width], 0.0).astype(jnp.bfloat16)
    values_out = jnp.where(valid3, kv_two[:, :, out_width:], 0.0).astype(jnp.bfloat16)

    length_me = jnp.take(lengths_here, core)
    prefix_scores = jnp.einsum(
        "htd,pd->htp", query, prefix_keys, preferred_element_type=jnp.float32
    ) * score_scale
    self_scores = jnp.einsum(
        "htd,sd->hts", query, key_rot, preferred_element_type=jnp.float32
    ) * score_scale
    self_allowed = (position[None, None, :] <= position[None, :, None]) & (
        position[None, None, :] < length_me
    )
    scores = jnp.concatenate([prefix_scores, self_scores], axis=2)
    allowed = jnp.concatenate(
        [jnp.ones(prefix_scores.shape, bool), jnp.broadcast_to(self_allowed, self_scores.shape)], axis=2
    )
    row_peak = jnp.max(jnp.where(allowed, scores, -jnp.inf), axis=2, keepdims=True)
    weights = jnp.where(allowed, jnp.exp(scores - row_peak), 0.0)
    total = jnp.sum(weights, axis=2, keepdims=True)
    all_values = jnp.concatenate([prefix_values, value], axis=0)
    numerator = jnp.einsum(
        "htk,kd->htd", weights.astype(jnp.bfloat16), all_values, preferred_element_type=jnp.float32
    )
    attention = (numerator / total).astype(jnp.bfloat16).transpose(1, 0, 2).reshape(L_MAX, 2 * HD)

    w_out_sib = lax.ppermute(w_out, "tensor", pair)
    w_out_chip = jnp.concatenate([w_out, w_out_sib], axis=0)
    attn_terms = jnp.dot(attention, w_out_chip, preferred_element_type=jnp.float32)
    sent = attn_terms.astype(jnp.bfloat16).reshape(L_MAX, tp_count, width_here).transpose(1, 0, 2)
    got = lax.all_to_all(sent, "tensor", 0, 0, tiled=True)
    attn_share = jnp.sum(
        got.reshape(tp_count // 2, local_reqs, L_MAX, width_here).astype(jnp.float32), axis=0
    ).reshape(row_count, width_here)
    middle = (state_shard.astype(jnp.float32) + attn_share).astype(jnp.bfloat16)
    w_gu_sib, w_down_sib = lax.ppermute(
        (jnp.concatenate([w_gate, w_up], axis=1), w_down), "tensor", pair
    )
    units = w_gate.shape[1]
    w_gate_chip = jnp.concatenate([w_gate, w_gu_sib[:, :units]], axis=1)
    w_up_chip = jnp.concatenate([w_up, w_gu_sib[:, units:]], axis=1)
    w_down_chip = jnp.concatenate([w_down, w_down_sib], axis=0)
    middle_req = middle.reshape(local_reqs, L_MAX, width_here)
    sent = jnp.take(middle_req, np.arange(tp_count) % 2, axis=0)
    got = lax.all_to_all(sent, "tensor", 0, 0, tiled=True)
    middle_rows = got.transpose(1, 0, 2).reshape(L_MAX, tp_count * width_here)
    normed_two = rms_scale(middle_rows.astype(jnp.float32), norm_mlp)
    gate = jnp.dot(normed_two, w_gate_chip, preferred_element_type=jnp.float32)
    upper = jnp.dot(normed_two, w_up_chip, preferred_element_type=jnp.float32)
    hidden = (jax.nn.silu(gate) * upper).astype(jnp.bfloat16)
    down_terms = jnp.dot(hidden, w_down_chip, preferred_element_type=jnp.float32)
    sent = down_terms.astype(jnp.bfloat16).reshape(L_MAX, tp_count, width_here).transpose(1, 0, 2)
    got = lax.all_to_all(sent, "tensor", 0, 0, tiled=True)
    down_share = jnp.sum(
        got.reshape(tp_count // 2, local_reqs, L_MAX, width_here).astype(jnp.float32), axis=0
    ).reshape(row_count, width_here)
    result = middle.astype(jnp.float32) + down_share
    result = (
        jnp.where(valid[:, None], result, 0.0)
        .astype(jnp.bfloat16)
        .reshape(local_reqs, L_MAX, width_here)
    )
    returned = lax.all_to_all(result, "dp", split_axis=1, concat_axis=0, tiled=True)
    hidden_out = jnp.zeros_like(returned).at[request_order].set(returned)
    return (hidden_out, keys_out, values_out)


def solution(mesh):
    in_specs = (
        P(None, "dp", "tensor"),
        P(),
        P(),
        P(),
        P(),
        P("dp", "tensor", None),
        P(),
        P(None, "tensor"),
        P(None, "tensor"),
        P(None, "tensor"),
        P("tensor", None),
        P(),
        P(None, "tensor"),
        P(None, "tensor"),
        P("tensor", None),
    )
    out_specs = (P(None, "dp", "tensor"), P("dp", None, "tensor"), P("dp", None, "tensor"))
    return jax.shard_map(shards, mesh=mesh, in_specs=in_specs, out_specs=out_specs, check_vma=False)
```

```python
import jax
import jax.numpy as jnp
import numpy as np
from jax import lax
from jax.sharding import PartitionSpec as P

H = 32
KVH = 8
HD = 64
L_MAX = 128
P_SIZE = 256


THETA = 10000000.0
EPSILON = 1e-05


def rms_scale(wide, gain):
    mean_square = jnp.mean(wide * wide, axis=-1, keepdims=True)
    return (wide * lax.rsqrt(mean_square + EPSILON) * gain.astype(jnp.float32)).astype(jnp.bfloat16)


def rotate(vectors, positions):
    half = HD // 2
    freqs = THETA ** (-(jnp.arange(half, dtype=jnp.float32) * 2.0 / HD))
    angles = positions[:, None] * freqs[None, :]
    cosine = jnp.cos(angles)
    sine = jnp.sin(angles)
    first = vectors[..., :half]
    second = vectors[..., half:]
    return jnp.concatenate(
        [first * cosine - second * sine, second * cosine + first * sine], axis=-1
    )


def gather_rows(shard, axis_name, count):
    sent = jnp.broadcast_to(shard[None], (count,) + shard.shape)
    got = lax.all_to_all(sent, axis_name, 0, 0, tiled=True)
    rows, width = shard.shape
    return got.transpose(1, 0, 2).reshape(rows, count * width)


def scatter_sum(terms, axis_name, count):
    rows, width = terms.shape
    share = width // count
    sent = terms.astype(jnp.bfloat16).reshape(rows, count, share).transpose(1, 0, 2)
    got = lax.all_to_all(sent, axis_name, 0, 0, tiled=True)
    return jnp.sum(got.astype(jnp.float32), axis=0)


def shards(
    suffix_states,
    suffix_lengths,
    request_group,
    group_owner,
    request_order,
    prefix_cache,
    norm_attn,
    w_query,
    w_key,
    w_value,
    w_out,
    norm_mlp,
    w_gate,
    w_up,
    w_down,
):
    dp_count = lax.axis_size("dp")
    tp_count = lax.axis_size("tensor")
    dp_index = lax.axis_index("dp")
    tp_index = lax.axis_index("tensor")
    total_reqs = suffix_lengths.shape[0]
    local_reqs = total_reqs // dp_count
    row_count = local_reqs * L_MAX
    heads_here = w_query.shape[1] // HD
    group_size = H // KVH
    assert heads_here == 1 and local_reqs == 2
    kv_cols = w_key.shape[1]
    d_here = kv_cols // KVH
    score_scale = HD ** (-0.5)
    kv_of_dest = np.arange(tp_count) * heads_here // group_size
    kv_here = tp_index * heads_here // group_size

    routed = jnp.take(suffix_states, request_order, axis=0)
    pos_here = routed.shape[1]
    width_here = routed.shape[2]
    state_part = routed.reshape(dp_count, local_reqs * pos_here * width_here)
    prefix_flat = prefix_cache.reshape(1, -1)
    prefix_part = jnp.broadcast_to(prefix_flat, (dp_count, prefix_flat.shape[1]))
    first = lax.all_to_all(
        jnp.concatenate([state_part, prefix_part], axis=1), "dp", 0, 0, tiled=True
    )
    state_split = state_part.shape[1]
    routed_here = (
        first[:, :state_split]
        .reshape(dp_count, local_reqs, pos_here, width_here)
        .transpose(1, 0, 2, 3)
        .reshape(local_reqs, dp_count * pos_here, width_here)
    )
    prefix_rows = prefix_cache.shape[1]
    prefix_all = first[:, state_split:].reshape(dp_count, prefix_rows, KVH, 2 * HD)

    state_shard = routed_here.reshape(row_count, width_here)
    req_ids = lax.dynamic_slice_in_dim(request_order, dp_index * local_reqs, local_reqs)
    hit = jnp.arange(total_reqs, dtype=jnp.int32)[None, :] == req_ids[:, None]
    lengths_here = jnp.sum(jnp.where(hit, suffix_lengths[None, :], 0), axis=1)
    group_here = jnp.sum(jnp.where(hit, request_group[:, 0][None, :], 0), axis=1)
    group_hit = jnp.arange(group_owner.shape[0], dtype=jnp.int32)[None, :] == group_here[:, None]
    owner_here = jnp.sum(jnp.where(group_hit, group_owner[None, :], 0), axis=1)
    position = jnp.arange(L_MAX, dtype=jnp.int32)
    valid = (position[None, :] < lengths_here[:, None]).reshape(row_count)
    positions = (P_SIZE + position).astype(jnp.float32)

    core = tp_index % 2
    pair = [(t, t ^ 1) for t in range(tp_count)]
    q_cols = w_query.shape[1]
    w_qkv_sib = lax.ppermute(jnp.concatenate([w_query, w_key, w_value], axis=1), "tensor", pair)
    w_query_chip = jnp.concatenate([w_query, w_qkv_sib[:, :q_cols]], axis=1)
    w_key_chip = jnp.concatenate([w_key, w_qkv_sib[:, q_cols : q_cols + kv_cols]], axis=1)
    w_value_chip = jnp.concatenate([w_value, w_qkv_sib[:, q_cols + kv_cols :]], axis=1)

    chosen = jnp.take(prefix_all, jnp.tile(owner_here, tp_count // 2), axis=0)
    chosen = jnp.take_along_axis(
        chosen, jnp.asarray(kv_of_dest).reshape(tp_count, 1, 1, 1), axis=2
    ).reshape(tp_count, prefix_rows, 2 * HD)

    state_req = routed_here
    sent = jnp.tile(state_req, (tp_count // 2, 1, 1))
    got = lax.all_to_all(sent, "tensor", 0, 0, tiled=True)
    full_rows = got.transpose(1, 0, 2).reshape(L_MAX, tp_count * width_here)
    normed = rms_scale(full_rows.astype(jnp.float32), norm_attn)
    query = jnp.dot(normed, w_query_chip, preferred_element_type=jnp.float32)
    query = query.reshape(L_MAX, 2 * heads_here, HD).transpose(1, 0, 2)
    query = rotate(query, positions).astype(jnp.bfloat16)
    kv_part = jnp.dot(
        normed, jnp.concatenate([w_key_chip, w_value_chip], axis=1), preferred_element_type=jnp.float32
    ).astype(jnp.bfloat16)
    chip_d = 2 * d_here
    pick = (np.arange(d_here)[None, :] * KVH + kv_of_dest[:, None])
    pick = np.concatenate(
        [pick, kv_cols + pick, 2 * kv_cols + pick, 3 * kv_cols + pick], axis=1
    )
    kv_all = jnp.concatenate(
        [kv_part[:, :kv_cols], kv_part[:, kv_cols : 2 * kv_cols],
         kv_part[:, 2 * kv_cols : 3 * kv_cols], kv_part[:, 3 * kv_cols :]], axis=1
    )
    kv_sent = jnp.take(kv_all, pick.reshape(-1), axis=1).reshape(L_MAX, tp_count, 2 * chip_d)
    prefix_split = chosen.shape[1] * chosen.shape[2]
    both = lax.all_to_all(
        jnp.concatenate(
            [chosen.reshape(tp_count, -1), kv_sent.transpose(1, 0, 2).reshape(tp_count, -1)],
            axis=1,
        ),
        "tensor", 0, 0, tiled=True,
    )
    picked = both[:, :prefix_split].reshape(tp_count, prefix_rows, 2 * HD)
    picked = picked.reshape(tp_count * prefix_rows, 2 * HD)
    prefix_keys = picked[:, :HD]
    prefix_values = picked[:, HD:]
    kv_got = both[:, prefix_split:].reshape(tp_count // 2, 2, L_MAX, 2 * chip_d)
    kv_got = jnp.take(kv_got, core, axis=1)
    src_t = (np.arange(tp_count // 2) * 2)[:, None]
    keys4 = kv_got[:, :, : 2 * d_here].reshape(tp_count // 2, L_MAX, 2, d_here)
    vals4 = kv_got[:, :, 2 * d_here :].reshape(tp_count // 2, L_MAX, 2, d_here)
    flip = core == 1
    keys4 = jnp.where(flip, keys4[:, :, ::-1], keys4)
    vals4 = jnp.where(flip, vals4[:, :, ::-1], vals4)
    key_raw = keys4.transpose(1, 0, 2, 3).reshape(L_MAX, HD)
    value = vals4.transpose(1, 0, 2, 3).reshape(L_MAX, HD)
    key_rot = rotate(key_raw.astype(jnp.float32), positions).astype(jnp.bfloat16)

    out_width = kv_cols
    out_first = (tp_index * out_width) % HD
    sib_first = ((tp_index ^ 1) * out_width) % HD
    kv_for_sib = jnp.concatenate(
        [lax.dynamic_slice_in_dim(key_rot, sib_first, out_width, 1),
         lax.dynamic_slice_in_dim(value, sib_first, out_width, 1)], axis=1
    )
    kv_from_sib = lax.ppermute(kv_for_sib, "tensor", pair)
    kv_mine = jnp.concatenate(
        [lax.dynamic_slice_in_dim(key_rot, out_first, out_width, 1),
         lax.dynamic_slice_in_dim(value, out_first, out_width, 1)], axis=1
    )
    kv_two = jnp.where(
        core == 0, jnp.stack([kv_mine, kv_from_sib]), jnp.stack([kv_from_sib, kv_mine])
    )
    valid3 = valid.reshape(local_reqs, L_MAX, 1)
    keys_out = jnp.where(valid3, kv_two[:, :, :out_width], 0.0).astype(jnp.bfloat16)
    values_out = jnp.where(valid3, kv_two[:, :, out_width:], 0.0).astype(jnp.bfloat16)

    length_me = jnp.take(lengths_here, core)
    prefix_scores = jnp.einsum(
        "htd,pd->htp", query, prefix_keys, preferred_element_type=jnp.float32
    ) * score_scale
    self_scores = jnp.einsum(
        "htd,sd->hts", query, key_rot, preferred_element_type=jnp.float32
    ) * score_scale
    self_allowed = (position[None, None, :] <= position[None, :, None]) & (
        position[None, None, :] < length_me
    )
    scores = jnp.concatenate([prefix_scores, self_scores], axis=2)
    allowed = jnp.concatenate(
        [jnp.ones(prefix_scores.shape, bool), jnp.broadcast_to(self_allowed, self_scores.shape)], axis=2
    )
    row_peak = jnp.max(jnp.where(allowed, scores, -jnp.inf), axis=2, keepdims=True)
    weights = jnp.where(allowed, jnp.exp(scores - row_peak), 0.0)
    total = jnp.sum(weights, axis=2, keepdims=True)
    all_values = jnp.concatenate([prefix_values, value], axis=0)
    numerator = jnp.einsum(
        "htk,kd->htd", weights.astype(jnp.bfloat16), all_values, preferred_element_type=jnp.float32
    )
    attention = (numerator / total).astype(jnp.bfloat16).transpose(1, 0, 2).reshape(L_MAX, 2 * HD)

    w_out_sib = lax.ppermute(w_out, "tensor", pair)
    w_out_chip = jnp.concatenate([w_out, w_out_sib], axis=0)
    attn_terms = jnp.dot(attention, w_out_chip, preferred_element_type=jnp.float32)
    sent = attn_terms.astype(jnp.bfloat16).reshape(L_MAX, tp_count, width_here).transpose(1, 0, 2)
    got = lax.all_to_all(sent, "tensor", 0, 0, tiled=True)
    attn_share = jnp.sum(
        got.reshape(tp_count // 2, local_reqs, L_MAX, width_here).astype(jnp.float32), axis=0
    ).reshape(row_count, width_here)
    middle = (state_shard.astype(jnp.float32) + attn_share).astype(jnp.bfloat16)
    w_gu_sib, w_down_sib = lax.ppermute(
        (jnp.concatenate([w_gate, w_up], axis=1), w_down), "tensor", pair
    )
    units = w_gate.shape[1]
    w_gate_chip = jnp.concatenate([w_gate, w_gu_sib[:, :units]], axis=1)
    w_up_chip = jnp.concatenate([w_up, w_gu_sib[:, units:]], axis=1)
    w_down_chip = jnp.concatenate([w_down, w_down_sib], axis=0)
    middle_req = middle.reshape(local_reqs, L_MAX, width_here)
    sent = jnp.tile(middle_req, (tp_count // 2, 1, 1))
    got = lax.all_to_all(sent, "tensor", 0, 0, tiled=True)
    middle_rows = got.transpose(1, 0, 2).reshape(L_MAX, tp_count * width_here)
    normed_two = rms_scale(middle_rows.astype(jnp.float32), norm_mlp)
    gate = jnp.dot(normed_two, w_gate_chip, preferred_element_type=jnp.float32)
    upper = jnp.dot(normed_two, w_up_chip, preferred_element_type=jnp.float32)
    hidden = (jax.nn.silu(gate) * upper).astype(jnp.bfloat16)
    down_terms = jnp.dot(hidden, w_down_chip, preferred_element_type=jnp.float32)
    sent = down_terms.astype(jnp.bfloat16).reshape(L_MAX, tp_count, width_here).transpose(1, 0, 2)
    got = lax.all_to_all(sent, "tensor", 0, 0, tiled=True)
    down_share = jnp.sum(
        got.reshape(tp_count // 2, local_reqs, L_MAX, width_here).astype(jnp.float32), axis=0
    ).reshape(row_count, width_here)
    result = middle.astype(jnp.float32) + down_share
    result = (
        jnp.where(valid[:, None], result, 0.0)
        .astype(jnp.bfloat16)
        .reshape(local_reqs, L_MAX, width_here)
    )
    returned = lax.all_to_all(result, "dp", split_axis=1, concat_axis=0, tiled=True)
    hidden_out = jnp.zeros_like(returned).at[request_order].set(returned)
    return (hidden_out, keys_out, values_out)


def solution(mesh):
    in_specs = (
        P(None, "dp", "tensor"),
        P(),
        P(),
        P(),
        P(),
        P("dp", "tensor", None),
        P(),
        P(None, "tensor"),
        P(None, "tensor"),
        P(None, "tensor"),
        P("tensor", None),
        P(),
        P(None, "tensor"),
        P(None, "tensor"),
        P("tensor", None),
    )
    out_specs = (P(None, "dp", "tensor"), P("dp", None, "tensor"), P("dp", None, "tensor"))
    return jax.shard_map(shards, mesh=mesh, in_specs=in_specs, out_specs=out_specs, check_vma=False)
```

```python
import jax
import jax.numpy as jnp
import numpy as np
from jax import lax
from jax.sharding import PartitionSpec as P

H = 32
KVH = 8
HD = 64
L_MAX = 128
P_SIZE = 256


THETA = 10000000.0
EPSILON = 1e-05


def rms_scale(wide, gain):
    mean_square = jnp.mean(wide * wide, axis=-1, keepdims=True)
    return (wide * lax.rsqrt(mean_square + EPSILON) * gain.astype(jnp.float32)).astype(jnp.bfloat16)


def rotate(vectors, positions):
    half = HD // 2
    freqs = THETA ** (-(jnp.arange(half, dtype=jnp.float32) * 2.0 / HD))
    angles = positions[:, None] * freqs[None, :]
    cosine = jnp.cos(angles)
    sine = jnp.sin(angles)
    first = vectors[..., :half]
    second = vectors[..., half:]
    return jnp.concatenate(
        [first * cosine - second * sine, second * cosine + first * sine], axis=-1
    )


def gather_rows(shard, axis_name, count):
    sent = jnp.broadcast_to(shard[None], (count,) + shard.shape)
    got = lax.all_to_all(sent, axis_name, 0, 0, tiled=True)
    rows, width = shard.shape
    return got.transpose(1, 0, 2).reshape(rows, count * width)


def scatter_sum(terms, axis_name, count):
    rows, width = terms.shape
    share = width // count
    sent = terms.astype(jnp.bfloat16).reshape(rows, count, share).transpose(1, 0, 2)
    got = lax.all_to_all(sent, axis_name, 0, 0, tiled=True)
    return jnp.sum(got.astype(jnp.float32), axis=0)


def shards(
    suffix_states,
    suffix_lengths,
    request_group,
    group_owner,
    request_order,
    prefix_cache,
    norm_attn,
    w_query,
    w_key,
    w_value,
    w_out,
    norm_mlp,
    w_gate,
    w_up,
    w_down,
):
    dp_count = lax.axis_size("dp")
    tp_count = lax.axis_size("tensor")
    dp_index = lax.axis_index("dp")
    tp_index = lax.axis_index("tensor")
    total_reqs = suffix_lengths.shape[0]
    local_reqs = total_reqs // dp_count
    row_count = local_reqs * L_MAX
    heads_here = w_query.shape[1] // HD
    group_size = H // KVH
    assert heads_here == 1 and local_reqs == 2
    kv_cols = w_key.shape[1]
    d_here = kv_cols // KVH
    score_scale = HD ** (-0.5)
    kv_of_dest = np.arange(tp_count) * heads_here // group_size
    kv_here = tp_index * heads_here // group_size

    routed = jnp.take(suffix_states, request_order, axis=0)
    pos_here = routed.shape[1]
    width_here = routed.shape[2]
    state_part = routed.reshape(dp_count, local_reqs * pos_here * width_here)
    prefix_flat = prefix_cache.reshape(1, -1)
    prefix_part = jnp.broadcast_to(prefix_flat, (dp_count, prefix_flat.shape[1]))
    first = lax.all_to_all(
        jnp.concatenate([state_part, prefix_part], axis=1), "dp", 0, 0, tiled=True
    )
    state_split = state_part.shape[1]
    routed_here = (
        first[:, :state_split]
        .reshape(dp_count, local_reqs, pos_here, width_here)
        .transpose(1, 0, 2, 3)
        .reshape(local_reqs, dp_count * pos_here, width_here)
    )
    prefix_rows = prefix_cache.shape[1]
    prefix_all = first[:, state_split:].reshape(dp_count, prefix_rows, KVH, 2 * HD)

    state_shard = routed_here.reshape(row_count, width_here)
    req_ids = lax.dynamic_slice_in_dim(request_order, dp_index * local_reqs, local_reqs)
    hit = jnp.arange(total_reqs, dtype=jnp.int32)[None, :] == req_ids[:, None]
    lengths_here = jnp.sum(jnp.where(hit, suffix_lengths[None, :], 0), axis=1)
    group_here = jnp.sum(jnp.where(hit, request_group[:, 0][None, :], 0), axis=1)
    group_hit = jnp.arange(group_owner.shape[0], dtype=jnp.int32)[None, :] == group_here[:, None]
    owner_here = jnp.sum(jnp.where(group_hit, group_owner[None, :], 0), axis=1)
    position = jnp.arange(L_MAX, dtype=jnp.int32)
    valid = (position[None, :] < lengths_here[:, None]).reshape(row_count)
    positions = (P_SIZE + position).astype(jnp.float32)

    core = tp_index % 2
    pair = [(t, t ^ 1) for t in range(tp_count)]
    q_cols = w_query.shape[1]
    w_qkv_sib = lax.ppermute(jnp.concatenate([w_query, w_key, w_value], axis=1), "tensor", pair)
    w_query_chip = jnp.concatenate([w_query, w_qkv_sib[:, :q_cols]], axis=1)
    w_key_chip = jnp.concatenate([w_key, w_qkv_sib[:, q_cols : q_cols + kv_cols]], axis=1)
    w_value_chip = jnp.concatenate([w_value, w_qkv_sib[:, q_cols + kv_cols :]], axis=1)

    per_kv = tp_count // KVH
    chosen = jnp.stack(
        [lax.dynamic_index_in_dim(prefix_all, owner_here[r], 0, keepdims=False) for r in range(local_reqs)]
    ).transpose(2, 0, 1, 3)
    chosen = jnp.broadcast_to(
        chosen[:, None], (KVH, per_kv // local_reqs) + chosen.shape[1:]
    ).reshape(tp_count, prefix_rows, 2 * HD)

    state_req = routed_here
    sent = jnp.tile(state_req, (tp_count // 2, 1, 1))
    got = lax.all_to_all(sent, "tensor", 0, 0, tiled=True)
    full_rows = got.transpose(1, 0, 2).reshape(L_MAX, tp_count * width_here)
    normed = rms_scale(full_rows.astype(jnp.float32), norm_attn)
    query = jnp.dot(normed, w_query_chip, preferred_element_type=jnp.float32)
    query = query.reshape(L_MAX, 2 * heads_here, HD).transpose(1, 0, 2)
    query = rotate(query, positions).astype(jnp.bfloat16)
    kv_part = jnp.dot(
        normed, jnp.concatenate([w_key_chip, w_value_chip], axis=1), preferred_element_type=jnp.float32
    ).astype(jnp.bfloat16)
    chip_d = 2 * d_here
    kv_sent = kv_part.reshape(L_MAX, 4, d_here, KVH).transpose(3, 0, 1, 2).reshape(KVH, L_MAX, 2 * chip_d)
    kv_sent = jnp.broadcast_to(kv_sent[:, None], (KVH, per_kv, L_MAX, 2 * chip_d)).reshape(
        tp_count, L_MAX, 2 * chip_d
    )
    prefix_split = chosen.shape[1] * chosen.shape[2]
    both = lax.all_to_all(
        jnp.concatenate(
            [chosen.reshape(tp_count, -1), kv_sent.reshape(tp_count, -1)],
            axis=1,
        ),
        "tensor", 0, 0, tiled=True,
    )
    picked = both[:, :prefix_split].reshape(tp_count, prefix_rows, 2 * HD)
    picked = picked.reshape(tp_count * prefix_rows, 2 * HD)
    prefix_keys = picked[:, :HD]
    prefix_values = picked[:, HD:]
    kv_got = both[:, prefix_split:].reshape(tp_count // 2, 2, L_MAX, 2 * chip_d)
    kv_got = jnp.take(kv_got, core, axis=1)
    src_t = (np.arange(tp_count // 2) * 2)[:, None]
    keys4 = kv_got[:, :, : 2 * d_here].reshape(tp_count // 2, L_MAX, 2, d_here)
    vals4 = kv_got[:, :, 2 * d_here :].reshape(tp_count // 2, L_MAX, 2, d_here)
    flip = core == 1
    keys4 = jnp.where(flip, keys4[:, :, ::-1], keys4)
    vals4 = jnp.where(flip, vals4[:, :, ::-1], vals4)
    key_raw = keys4.transpose(1, 0, 2, 3).reshape(L_MAX, HD)
    value = vals4.transpose(1, 0, 2, 3).reshape(L_MAX, HD)
    key_rot = rotate(key_raw.astype(jnp.float32), positions).astype(jnp.bfloat16)

    out_width = kv_cols
    out_first = (tp_index * out_width) % HD
    sib_first = ((tp_index ^ 1) * out_width) % HD
    kv_for_sib = jnp.concatenate(
        [lax.dynamic_slice_in_dim(key_rot, sib_first, out_width, 1),
         lax.dynamic_slice_in_dim(value, sib_first, out_width, 1)], axis=1
    )
    kv_from_sib = lax.ppermute(kv_for_sib, "tensor", pair)
    kv_mine = jnp.concatenate(
        [lax.dynamic_slice_in_dim(key_rot, out_first, out_width, 1),
         lax.dynamic_slice_in_dim(value, out_first, out_width, 1)], axis=1
    )
    kv_two = jnp.where(
        core == 0, jnp.stack([kv_mine, kv_from_sib]), jnp.stack([kv_from_sib, kv_mine])
    )
    valid3 = valid.reshape(local_reqs, L_MAX, 1)
    keys_out = jnp.where(valid3, kv_two[:, :, :out_width], 0.0).astype(jnp.bfloat16)
    values_out = jnp.where(valid3, kv_two[:, :, out_width:], 0.0).astype(jnp.bfloat16)

    length_me = jnp.take(lengths_here, core)
    prefix_scores = jnp.einsum(
        "htd,pd->htp", query, prefix_keys, preferred_element_type=jnp.float32
    ) * score_scale
    self_scores = jnp.einsum(
        "htd,sd->hts", query, key_rot, preferred_element_type=jnp.float32
    ) * score_scale
    self_allowed = (position[None, None, :] <= position[None, :, None]) & (
        position[None, None, :] < length_me
    )
    scores = jnp.concatenate([prefix_scores, self_scores], axis=2)
    allowed = jnp.concatenate(
        [jnp.ones(prefix_scores.shape, bool), jnp.broadcast_to(self_allowed, self_scores.shape)], axis=2
    )
    row_peak = jnp.max(jnp.where(allowed, scores, -jnp.inf), axis=2, keepdims=True)
    weights = jnp.where(allowed, jnp.exp(scores - row_peak), 0.0)
    total = jnp.sum(weights, axis=2, keepdims=True)
    all_values = jnp.concatenate([prefix_values, value], axis=0)
    numerator = jnp.einsum(
        "htk,kd->htd", weights.astype(jnp.bfloat16), all_values, preferred_element_type=jnp.float32
    )
    attention = (numerator / total).astype(jnp.bfloat16).transpose(1, 0, 2).reshape(L_MAX, 2 * HD)

    w_out_sib = lax.ppermute(w_out, "tensor", pair)
    w_out_chip = jnp.concatenate([w_out, w_out_sib], axis=0)
    attn_terms = jnp.dot(attention, w_out_chip, preferred_element_type=jnp.float32)
    sent = attn_terms.astype(jnp.bfloat16).reshape(L_MAX, tp_count, width_here).transpose(1, 0, 2)
    got = lax.all_to_all(sent, "tensor", 0, 0, tiled=True)
    attn_share = jnp.sum(
        got.reshape(tp_count // 2, local_reqs, L_MAX, width_here).astype(jnp.float32), axis=0
    ).reshape(row_count, width_here)
    middle = (state_shard.astype(jnp.float32) + attn_share).astype(jnp.bfloat16)
    w_gu_sib, w_down_sib = lax.ppermute(
        (jnp.concatenate([w_gate, w_up], axis=1), w_down), "tensor", pair
    )
    units = w_gate.shape[1]
    w_gate_chip = jnp.concatenate([w_gate, w_gu_sib[:, :units]], axis=1)
    w_up_chip = jnp.concatenate([w_up, w_gu_sib[:, units:]], axis=1)
    w_down_chip = jnp.concatenate([w_down, w_down_sib], axis=0)
    middle_req = middle.reshape(local_reqs, L_MAX, width_here)
    sent = jnp.tile(middle_req, (tp_count // 2, 1, 1))
    got = lax.all_to_all(sent, "tensor", 0, 0, tiled=True)
    middle_rows = got.transpose(1, 0, 2).reshape(L_MAX, tp_count * width_here)
    normed_two = rms_scale(middle_rows.astype(jnp.float32), norm_mlp)
    gate = jnp.dot(normed_two, w_gate_chip, preferred_element_type=jnp.float32)
    upper = jnp.dot(normed_two, w_up_chip, preferred_element_type=jnp.float32)
    hidden = (jax.nn.silu(gate) * upper).astype(jnp.bfloat16)
    down_terms = jnp.dot(hidden, w_down_chip, preferred_element_type=jnp.float32)
    sent = down_terms.astype(jnp.bfloat16).reshape(L_MAX, tp_count, width_here).transpose(1, 0, 2)
    got = lax.all_to_all(sent, "tensor", 0, 0, tiled=True)
    down_share = jnp.sum(
        got.reshape(tp_count // 2, local_reqs, L_MAX, width_here).astype(jnp.float32), axis=0
    ).reshape(row_count, width_here)
    result = middle.astype(jnp.float32) + down_share
    result = (
        jnp.where(valid[:, None], result, 0.0)
        .astype(jnp.bfloat16)
        .reshape(local_reqs, L_MAX, width_here)
    )
    returned = lax.all_to_all(result, "dp", split_axis=1, concat_axis=0, tiled=True)
    hidden_out = jnp.zeros_like(returned).at[request_order].set(returned)
    return (hidden_out, keys_out, values_out)


def solution(mesh):
    in_specs = (
        P(None, "dp", "tensor"),
        P(),
        P(),
        P(),
        P(),
        P("dp", "tensor", None),
        P(),
        P(None, "tensor"),
        P(None, "tensor"),
        P(None, "tensor"),
        P("tensor", None),
        P(),
        P(None, "tensor"),
        P(None, "tensor"),
        P("tensor", None),
    )
    out_specs = (P(None, "dp", "tensor"), P("dp", None, "tensor"), P("dp", None, "tensor"))
    return jax.shard_map(shards, mesh=mesh, in_specs=in_specs, out_specs=out_specs, check_vma=False)
```

```python
import jax
import jax.numpy as jnp
from jax import lax
from jax.sharding import PartitionSpec as P

KVH = 8
HD = 64
L_MAX = 128
P_SIZE = 256


THETA = 10000000.0
EPSILON = 1e-05


def rms_scale(wide, gain):
    mean_square = jnp.mean(wide * wide, axis=-1, keepdims=True)
    return (wide * lax.rsqrt(mean_square + EPSILON) * gain.astype(jnp.float32)).astype(jnp.bfloat16)


def rotate(vectors, positions):
    half = HD // 2
    freqs = THETA ** (-(jnp.arange(half, dtype=jnp.float32) * 2.0 / HD))
    angles = positions[:, None] * freqs[None, :]
    cosine = jnp.cos(angles)
    sine = jnp.sin(angles)
    first = vectors[..., :half]
    second = vectors[..., half:]
    return jnp.concatenate(
        [first * cosine - second * sine, second * cosine + first * sine], axis=-1
    )


def layer(
    suffix_states,
    suffix_lengths,
    request_group,
    group_owner,
    request_order,
    prefix_cache,
    norm_attn,
    w_query,
    w_key,
    w_value,
    w_out,
    norm_mlp,
    w_gate,
    w_up,
    w_down,
):
    dp_count = lax.axis_size("dp")
    tp_count = lax.axis_size("tensor")
    dp_index = lax.axis_index("dp")
    tp_index = lax.axis_index("tensor")
    total_reqs = suffix_lengths.shape[0]
    local_reqs = total_reqs // dp_count
    row_count = local_reqs * L_MAX
    heads_here = w_query.shape[1] // HD
    assert heads_here == 1 and local_reqs == 2
    kv_cols = w_key.shape[1]
    d_here = kv_cols // KVH
    score_scale = HD ** (-0.5)

    routed = jnp.take(suffix_states, request_order, axis=0)
    pos_here = routed.shape[1]
    width_here = routed.shape[2]
    state_part = routed.reshape(dp_count, local_reqs * pos_here * width_here)
    prefix_flat = prefix_cache.reshape(1, -1)
    prefix_part = jnp.broadcast_to(prefix_flat, (dp_count, prefix_flat.shape[1]))
    first = lax.all_to_all(
        jnp.concatenate([state_part, prefix_part], axis=1), "dp", 0, 0, tiled=True
    )
    state_split = state_part.shape[1]
    routed_here = (
        first[:, :state_split]
        .reshape(dp_count, local_reqs, pos_here, width_here)
        .transpose(1, 0, 2, 3)
        .reshape(local_reqs, dp_count * pos_here, width_here)
    )
    prefix_rows = prefix_cache.shape[1]
    prefix_all = first[:, state_split:].reshape(dp_count, prefix_rows, KVH, 2 * HD)

    state_shard = routed_here.reshape(row_count, width_here)
    req_ids = lax.dynamic_slice_in_dim(request_order, dp_index * local_reqs, local_reqs)
    hit = jnp.arange(total_reqs, dtype=jnp.int32)[None, :] == req_ids[:, None]
    lengths_here = jnp.sum(jnp.where(hit, suffix_lengths[None, :], 0), axis=1)
    group_here = jnp.sum(jnp.where(hit, request_group[:, 0][None, :], 0), axis=1)
    group_hit = jnp.arange(group_owner.shape[0], dtype=jnp.int32)[None, :] == group_here[:, None]
    owner_here = jnp.sum(jnp.where(group_hit, group_owner[None, :], 0), axis=1)
    position = jnp.arange(L_MAX, dtype=jnp.int32)
    valid = (position[None, :] < lengths_here[:, None]).reshape(row_count)
    positions = (P_SIZE + position).astype(jnp.float32)

    core = tp_index % 2
    pair = [(t, t ^ 1) for t in range(tp_count)]
    q_cols = w_query.shape[1]
    w_qkv_sib = lax.ppermute(jnp.concatenate([w_query, w_key, w_value], axis=1), "tensor", pair)
    w_query_chip = jnp.concatenate([w_query, w_qkv_sib[:, :q_cols]], axis=1)
    w_key_chip = jnp.concatenate([w_key, w_qkv_sib[:, q_cols : q_cols + kv_cols]], axis=1)
    w_value_chip = jnp.concatenate([w_value, w_qkv_sib[:, q_cols + kv_cols :]], axis=1)

    per_kv = tp_count // KVH
    chosen = jnp.stack(
        [lax.dynamic_index_in_dim(prefix_all, owner_here[r], 0, keepdims=False) for r in range(local_reqs)]
    ).transpose(2, 0, 1, 3)
    chosen = jnp.broadcast_to(
        chosen[:, None], (KVH, per_kv // local_reqs) + chosen.shape[1:]
    ).reshape(tp_count, prefix_rows, 2 * HD)

    state_req = routed_here
    sent = jnp.tile(state_req, (tp_count // 2, 1, 1))
    got = lax.all_to_all(sent, "tensor", 0, 0, tiled=True)
    full_rows = got.transpose(1, 0, 2).reshape(L_MAX, tp_count * width_here)
    normed = rms_scale(full_rows.astype(jnp.float32), norm_attn)
    query = jnp.dot(normed, w_query_chip, preferred_element_type=jnp.float32)
    query = query.reshape(L_MAX, 2 * heads_here, HD).transpose(1, 0, 2)
    query = rotate(query, positions).astype(jnp.bfloat16)
    kv_part = jnp.dot(
        normed, jnp.concatenate([w_key_chip, w_value_chip], axis=1), preferred_element_type=jnp.float32
    ).astype(jnp.bfloat16)
    chip_d = 2 * d_here
    kv_sent = kv_part.reshape(L_MAX, 4, d_here, KVH).transpose(3, 0, 1, 2).reshape(KVH, L_MAX, 2 * chip_d)
    kv_sent = jnp.broadcast_to(kv_sent[:, None], (KVH, per_kv, L_MAX, 2 * chip_d)).reshape(
        tp_count, L_MAX, 2 * chip_d
    )
    prefix_split = chosen.shape[1] * chosen.shape[2]
    packed = jnp.concatenate([chosen.reshape(tp_count, -1), kv_sent.reshape(tp_count, -1)], axis=1)
    both = lax.all_to_all(packed, "tensor", 0, 0, tiled=True)
    picked = both[:, :prefix_split].reshape(tp_count, prefix_rows, 2 * HD)
    picked = picked.reshape(tp_count * prefix_rows, 2 * HD)
    prefix_keys = picked[:, :HD]
    prefix_values = picked[:, HD:]
    kv_got = both[:, prefix_split:].reshape(tp_count // 2, 2, L_MAX, 2 * chip_d)
    kv_got = jnp.take(kv_got, core, axis=1)
    keys4 = kv_got[:, :, : 2 * d_here].reshape(tp_count // 2, L_MAX, 2, d_here)
    vals4 = kv_got[:, :, 2 * d_here :].reshape(tp_count // 2, L_MAX, 2, d_here)
    flip = core == 1
    keys4 = jnp.where(flip, keys4[:, :, ::-1], keys4)
    vals4 = jnp.where(flip, vals4[:, :, ::-1], vals4)
    key_raw = keys4.transpose(1, 0, 2, 3).reshape(L_MAX, HD)
    value = vals4.transpose(1, 0, 2, 3).reshape(L_MAX, HD)
    key_rot = rotate(key_raw.astype(jnp.float32), positions).astype(jnp.bfloat16)

    out_width = kv_cols
    out_first = (tp_index * out_width) % HD
    sib_first = ((tp_index ^ 1) * out_width) % HD
    kv_for_sib = jnp.concatenate(
        [lax.dynamic_slice_in_dim(key_rot, sib_first, out_width, 1),
         lax.dynamic_slice_in_dim(value, sib_first, out_width, 1)], axis=1
    )
    kv_from_sib = lax.ppermute(kv_for_sib, "tensor", pair)
    kv_mine = jnp.concatenate(
        [lax.dynamic_slice_in_dim(key_rot, out_first, out_width, 1),
         lax.dynamic_slice_in_dim(value, out_first, out_width, 1)], axis=1
    )
    kv_two = jnp.where(
        core == 0, jnp.stack([kv_mine, kv_from_sib]), jnp.stack([kv_from_sib, kv_mine])
    )
    valid3 = valid.reshape(local_reqs, L_MAX, 1)
    keys_out = jnp.where(valid3, kv_two[:, :, :out_width], 0.0).astype(jnp.bfloat16)
    values_out = jnp.where(valid3, kv_two[:, :, out_width:], 0.0).astype(jnp.bfloat16)

    length_me = jnp.take(lengths_here, core)
    prefix_scores = jnp.einsum(
        "htd,pd->htp", query, prefix_keys, preferred_element_type=jnp.float32
    ) * score_scale
    self_scores = jnp.einsum(
        "htd,sd->hts", query, key_rot, preferred_element_type=jnp.float32
    ) * score_scale
    self_allowed = (position[None, None, :] <= position[None, :, None]) & (
        position[None, None, :] < length_me
    )
    scores = jnp.concatenate([prefix_scores, self_scores], axis=2)
    allowed = jnp.concatenate(
        [jnp.ones(prefix_scores.shape, bool), jnp.broadcast_to(self_allowed, self_scores.shape)], axis=2
    )
    row_peak = jnp.max(jnp.where(allowed, scores, -jnp.inf), axis=2, keepdims=True)
    weights = jnp.where(allowed, jnp.exp(scores - row_peak), 0.0)
    total = jnp.sum(weights, axis=2, keepdims=True)
    all_values = jnp.concatenate([prefix_values, value], axis=0)
    numerator = jnp.einsum(
        "htk,kd->htd", weights.astype(jnp.bfloat16), all_values, preferred_element_type=jnp.float32
    )
    attention = (numerator / total).astype(jnp.bfloat16).transpose(1, 0, 2).reshape(L_MAX, 2 * HD)

    w_out_sib = lax.ppermute(w_out, "tensor", pair)
    w_out_chip = jnp.concatenate([w_out, w_out_sib], axis=0)
    attn_terms = jnp.dot(attention, w_out_chip, preferred_element_type=jnp.float32)
    sent = attn_terms.astype(jnp.bfloat16).reshape(L_MAX, tp_count, width_here).transpose(1, 0, 2)
    got = lax.all_to_all(sent, "tensor", 0, 0, tiled=True)
    attn_share = jnp.sum(
        got.reshape(tp_count // 2, local_reqs, L_MAX, width_here).astype(jnp.float32), axis=0
    ).reshape(row_count, width_here)
    middle = (state_shard.astype(jnp.float32) + attn_share).astype(jnp.bfloat16)
    w_gu_sib, w_down_sib = lax.ppermute(
        (jnp.concatenate([w_gate, w_up], axis=1), w_down), "tensor", pair
    )
    units = w_gate.shape[1]
    w_gate_chip = jnp.concatenate([w_gate, w_gu_sib[:, :units]], axis=1)
    w_up_chip = jnp.concatenate([w_up, w_gu_sib[:, units:]], axis=1)
    w_down_chip = jnp.concatenate([w_down, w_down_sib], axis=0)
    middle_req = middle.reshape(local_reqs, L_MAX, width_here)
    sent = jnp.tile(middle_req, (tp_count // 2, 1, 1))
    got = lax.all_to_all(sent, "tensor", 0, 0, tiled=True)
    middle_rows = got.transpose(1, 0, 2).reshape(L_MAX, tp_count * width_here)
    normed_two = rms_scale(middle_rows.astype(jnp.float32), norm_mlp)
    gate = jnp.dot(normed_two, w_gate_chip, preferred_element_type=jnp.float32)
    upper = jnp.dot(normed_two, w_up_chip, preferred_element_type=jnp.float32)
    hidden = (jax.nn.silu(gate) * upper).astype(jnp.bfloat16)
    down_terms = jnp.dot(hidden, w_down_chip, preferred_element_type=jnp.float32)
    sent = down_terms.astype(jnp.bfloat16).reshape(L_MAX, tp_count, width_here).transpose(1, 0, 2)
    got = lax.all_to_all(sent, "tensor", 0, 0, tiled=True)
    down_share = jnp.sum(
        got.reshape(tp_count // 2, local_reqs, L_MAX, width_here).astype(jnp.float32), axis=0
    ).reshape(row_count, width_here)
    result = middle.astype(jnp.float32) + down_share
    result = (
        jnp.where(valid[:, None], result, 0.0)
        .astype(jnp.bfloat16)
        .reshape(local_reqs, L_MAX, width_here)
    )
    returned = lax.all_to_all(result, "dp", split_axis=1, concat_axis=0, tiled=True)
    hidden_out = jnp.zeros_like(returned).at[request_order].set(returned)
    return (hidden_out, keys_out, values_out)


def solution(mesh):
    in_specs = (
        P(None, "dp", "tensor"),
        P(),
        P(),
        P(),
        P(),
        P("dp", "tensor", None),
        P(),
        P(None, "tensor"),
        P(None, "tensor"),
        P(None, "tensor"),
        P("tensor", None),
        P(),
        P(None, "tensor"),
        P(None, "tensor"),
        P("tensor", None),
    )
    out_specs = (P(None, "dp", "tensor"), P("dp", None, "tensor"), P("dp", None, "tensor"))
    return jax.shard_map(layer, mesh=mesh, in_specs=in_specs, out_specs=out_specs, check_vma=False)
```

```python
import jax
import jax.numpy as jnp
from jax import lax
from jax.sharding import PartitionSpec as P

KVH = 8
HD = 64
L_MAX = 128
P_SIZE = 256


THETA = 10000000.0
EPSILON = 1e-05


def rms_scale(wide, gain):
    mean_square = jnp.mean(wide * wide, axis=-1, keepdims=True)
    return (wide * lax.rsqrt(mean_square + EPSILON) * gain.astype(jnp.float32)).astype(jnp.bfloat16)


def rotate(vectors, positions):
    half = HD // 2
    freqs = THETA ** (-(jnp.arange(half, dtype=jnp.float32) * 2.0 / HD))
    angles = positions[:, None] * freqs[None, :]
    cosine = jnp.cos(angles)
    sine = jnp.sin(angles)
    first = vectors[..., :half]
    second = vectors[..., half:]
    return jnp.concatenate(
        [first * cosine - second * sine, second * cosine + first * sine], axis=-1
    )


def layer(
    suffix_states,
    suffix_lengths,
    request_group,
    group_owner,
    request_order,
    prefix_cache,
    norm_attn,
    w_query,
    w_key,
    w_value,
    w_out,
    norm_mlp,
    w_gate,
    w_up,
    w_down,
):
    dp_count = lax.axis_size("dp")
    tp_count = lax.axis_size("tensor")
    dp_index = lax.axis_index("dp")
    tp_index = lax.axis_index("tensor")
    total_reqs = suffix_lengths.shape[0]
    local_reqs = total_reqs // dp_count
    row_count = local_reqs * L_MAX
    heads_here = w_query.shape[1] // HD
    assert heads_here == 1 and local_reqs == 2
    kv_cols = w_key.shape[1]
    d_here = kv_cols // KVH
    score_scale = HD ** (-0.5)

    routed = jnp.take(suffix_states, request_order, axis=0)
    pos_here = routed.shape[1]
    width_here = routed.shape[2]
    state_part = routed.reshape(dp_count, local_reqs * pos_here * width_here)
    prefix_flat = prefix_cache.reshape(1, -1)
    prefix_part = jnp.broadcast_to(prefix_flat, (dp_count, prefix_flat.shape[1]))
    first = lax.all_to_all(
        jnp.concatenate([state_part, prefix_part], axis=1), "dp", 0, 0, tiled=True
    )
    state_split = state_part.shape[1]
    routed_here = (
        first[:, :state_split]
        .reshape(dp_count, local_reqs, pos_here, width_here)
        .transpose(1, 0, 2, 3)
        .reshape(local_reqs, dp_count * pos_here, width_here)
    )
    prefix_rows = prefix_cache.shape[1]
    prefix_all = first[:, state_split:].reshape(dp_count, prefix_rows, KVH, 2 * HD)

    state_shard = routed_here.reshape(row_count, width_here)
    req_ids = lax.dynamic_slice_in_dim(request_order, dp_index * local_reqs, local_reqs)
    hit = jnp.arange(total_reqs, dtype=jnp.int32)[None, :] == req_ids[:, None]
    lengths_here = jnp.sum(jnp.where(hit, suffix_lengths[None, :], 0), axis=1)
    group_here = jnp.sum(jnp.where(hit, request_group[:, 0][None, :], 0), axis=1)
    group_hit = jnp.arange(group_owner.shape[0], dtype=jnp.int32)[None, :] == group_here[:, None]
    owner_here = jnp.sum(jnp.where(group_hit, group_owner[None, :], 0), axis=1)
    position = jnp.arange(L_MAX, dtype=jnp.int32)
    valid = (position[None, :] < lengths_here[:, None]).reshape(row_count)
    positions = (P_SIZE + position).astype(jnp.float32)

    core = tp_index % 2
    pair = [(t, t ^ 1) for t in range(tp_count)]
    q_cols = w_query.shape[1]
    w_qkv_sib = lax.ppermute(jnp.concatenate([w_query, w_key, w_value], axis=1), "tensor", pair)
    w_query_chip = jnp.concatenate([w_query, w_qkv_sib[:, :q_cols]], axis=1)
    w_key_chip = jnp.concatenate([w_key, w_qkv_sib[:, q_cols : q_cols + kv_cols]], axis=1)
    w_value_chip = jnp.concatenate([w_value, w_qkv_sib[:, q_cols + kv_cols :]], axis=1)

    per_kv = tp_count // KVH
    chosen = jnp.stack(
        [lax.dynamic_index_in_dim(prefix_all, owner_here[r], 0, keepdims=False) for r in range(local_reqs)]
    ).transpose(2, 0, 1, 3)
    chosen = jnp.broadcast_to(
        chosen[:, None], (KVH, per_kv // local_reqs) + chosen.shape[1:]
    ).reshape(tp_count, prefix_rows, 2 * HD)

    state_req = routed_here
    sent = jnp.tile(state_req, (tp_count // 2, 1, 1))
    got = lax.all_to_all(sent, "tensor", 0, 0, tiled=True)
    full_rows = got.transpose(1, 0, 2).reshape(L_MAX, tp_count * width_here)
    normed = rms_scale(full_rows.astype(jnp.float32), norm_attn)
    query = jnp.dot(normed, w_query_chip, preferred_element_type=jnp.float32)
    query = query.reshape(L_MAX, 2 * heads_here, HD).transpose(1, 0, 2)
    query = rotate(query, positions).astype(jnp.bfloat16)
    kv_part = jnp.dot(
        normed, jnp.concatenate([w_key_chip, w_value_chip], axis=1), preferred_element_type=jnp.float32
    ).astype(jnp.bfloat16)
    chip_d = 2 * d_here
    kv_sent = kv_part.reshape(L_MAX, 4, d_here, KVH).transpose(3, 0, 1, 2).reshape(KVH, L_MAX, 2 * chip_d)
    kv_sent = jnp.broadcast_to(kv_sent[:, None], (KVH, per_kv, L_MAX, 2 * chip_d)).reshape(
        tp_count, L_MAX, 2 * chip_d
    )
    prefix_split = chosen.shape[1] * chosen.shape[2]
    packed = jnp.concatenate([chosen.reshape(tp_count, -1), kv_sent.reshape(tp_count, -1)], axis=1)
    both = lax.all_to_all(packed, "tensor", 0, 0, tiled=True)
    picked = both[:, :prefix_split].reshape(tp_count, prefix_rows, 2 * HD)
    picked = picked.reshape(tp_count * prefix_rows, 2 * HD)
    prefix_keys = picked[:, :HD]
    prefix_values = picked[:, HD:]
    kv_got = both[:, prefix_split:].reshape(tp_count // 2, 2, L_MAX, 2 * chip_d)
    kv_got = jnp.take(kv_got, core, axis=1)
    keys4 = kv_got[:, :, : 2 * d_here].reshape(tp_count // 2, L_MAX, 2, d_here)
    vals4 = kv_got[:, :, 2 * d_here :].reshape(tp_count // 2, L_MAX, 2, d_here)
    flip = core == 1
    keys4 = jnp.where(flip, keys4[:, :, ::-1], keys4)
    vals4 = jnp.where(flip, vals4[:, :, ::-1], vals4)
    key_raw = keys4.transpose(1, 0, 2, 3).reshape(L_MAX, HD)
    value = vals4.transpose(1, 0, 2, 3).reshape(L_MAX, HD)
    key_rot = rotate(key_raw.astype(jnp.float32), positions).astype(jnp.bfloat16)

    out_width = kv_cols
    out_first = (tp_index * out_width) % HD
    sib_first = ((tp_index ^ 1) * out_width) % HD
    kv_for_sib = jnp.concatenate(
        [lax.dynamic_slice_in_dim(key_rot, sib_first, out_width, 1),
         lax.dynamic_slice_in_dim(value, sib_first, out_width, 1)], axis=1
    )
    kv_from_sib = lax.ppermute(kv_for_sib, "tensor", pair)
    kv_mine = jnp.concatenate(
        [lax.dynamic_slice_in_dim(key_rot, out_first, out_width, 1),
         lax.dynamic_slice_in_dim(value, out_first, out_width, 1)], axis=1
    )
    kv_two = jnp.where(
        core == 0, jnp.stack([kv_mine, kv_from_sib]), jnp.stack([kv_from_sib, kv_mine])
    )
    valid3 = valid.reshape(local_reqs, L_MAX, 1)
    keys_out = jnp.where(valid3, kv_two[:, :, :out_width], 0.0).astype(jnp.bfloat16)
    values_out = jnp.where(valid3, kv_two[:, :, out_width:], 0.0).astype(jnp.bfloat16)

    length_me = jnp.take(lengths_here, core)
    prefix_scores = jnp.einsum(
        "htd,pd->htp", query, prefix_keys, preferred_element_type=jnp.float32
    ) * score_scale
    self_scores = jnp.einsum(
        "htd,sd->hts", query, key_rot, preferred_element_type=jnp.float32
    ) * score_scale
    self_allowed = (position[None, None, :] <= position[None, :, None]) & (
        position[None, None, :] < length_me
    )
    scores = jnp.concatenate([prefix_scores, self_scores], axis=2)
    allowed = jnp.concatenate(
        [jnp.ones(prefix_scores.shape, bool), jnp.broadcast_to(self_allowed, self_scores.shape)], axis=2
    )
    row_peak = jnp.max(jnp.where(allowed, scores, -jnp.inf), axis=2, keepdims=True)
    weights = jnp.where(allowed, jnp.exp(scores - row_peak), 0.0)
    total = jnp.sum(weights, axis=2, keepdims=True)
    all_values = jnp.concatenate([prefix_values, value], axis=0)
    numerator = jnp.einsum(
        "htk,kd->htd", weights.astype(jnp.bfloat16), all_values, preferred_element_type=jnp.float32
    )
    attention = (numerator / total).astype(jnp.bfloat16).transpose(1, 0, 2).reshape(L_MAX, 2 * HD)

    w_out_sib = lax.ppermute(w_out, "tensor", pair)
    w_out_chip = jnp.concatenate([w_out, w_out_sib], axis=0)
    attn_terms = jnp.dot(attention, w_out_chip, preferred_element_type=jnp.float32)
    sent = attn_terms.astype(jnp.bfloat16).reshape(L_MAX, tp_count, width_here).transpose(1, 0, 2)
    got = lax.all_to_all(sent, "tensor", 0, 0, tiled=True)
    attn_share = jnp.sum(
        got.reshape(tp_count // 2, local_reqs, L_MAX, width_here).astype(jnp.float32), axis=0
    ).reshape(row_count, width_here)
    middle = (state_shard.astype(jnp.float32) + attn_share).astype(jnp.bfloat16)
    w_gu_sib, w_down_sib = lax.ppermute(
        (jnp.concatenate([w_gate, w_up], axis=1), w_down), "tensor", pair
    )
    units = w_gate.shape[1]
    w_gate_chip = jnp.concatenate([w_gate, w_gu_sib[:, :units]], axis=1)
    w_up_chip = jnp.concatenate([w_up, w_gu_sib[:, units:]], axis=1)
    w_down_chip = jnp.concatenate([w_down, w_down_sib], axis=0)
    middle_req = middle.reshape(local_reqs, L_MAX, width_here)
    sent = jnp.tile(middle_req, (tp_count // 2, 1, 1))
    got = lax.all_to_all(sent, "tensor", 0, 0, tiled=True)
    middle_rows = got.transpose(1, 0, 2).reshape(L_MAX, tp_count * width_here)
    normed_two = rms_scale(middle_rows.astype(jnp.float32), norm_mlp)
    gate = jnp.dot(normed_two, w_gate_chip, preferred_element_type=jnp.float32)
    upper = jnp.dot(normed_two, w_up_chip, preferred_element_type=jnp.float32)
    hidden = (jax.nn.silu(gate) * upper).astype(jnp.bfloat16)
    down_terms = jnp.dot(hidden, w_down_chip, preferred_element_type=jnp.float32)
    sent = down_terms.astype(jnp.bfloat16).reshape(L_MAX, tp_count, width_here).transpose(1, 0, 2)
    got = lax.all_to_all(sent, "tensor", 0, 0, tiled=True)
    down_share = jnp.sum(
        got.reshape(tp_count // 2, local_reqs, L_MAX, width_here).astype(jnp.float32), axis=0
    ).reshape(row_count, width_here)
    result = middle.astype(jnp.float32) + down_share
    result = (
        jnp.where(valid[:, None], result, 0.0)
        .astype(jnp.bfloat16)
        .reshape(local_reqs, L_MAX, width_here)
    )
    returned = lax.all_to_all(result, "dp", split_axis=1, concat_axis=0, tiled=True)
    order_hit = (
        jnp.arange(total_reqs, dtype=jnp.int32)[:, None] == request_order[None, :]
    ).astype(jnp.bfloat16)
    hidden_out = jnp.dot(
        order_hit, returned.reshape(total_reqs, -1), preferred_element_type=jnp.float32
    ).astype(jnp.bfloat16).reshape(returned.shape)
    return (hidden_out, keys_out, values_out)


def solution(mesh):
    in_specs = (
        P(None, "dp", "tensor"),
        P(),
        P(),
        P(),
        P(),
        P("dp", "tensor", None),
        P(),
        P(None, "tensor"),
        P(None, "tensor"),
        P(None, "tensor"),
        P("tensor", None),
        P(),
        P(None, "tensor"),
        P(None, "tensor"),
        P("tensor", None),
    )
    out_specs = (P(None, "dp", "tensor"), P("dp", None, "tensor"), P("dp", None, "tensor"))
    return jax.shard_map(layer, mesh=mesh, in_specs=in_specs, out_specs=out_specs, check_vma=False)
```

```python
import jax
import jax.numpy as jnp
from jax import lax
from jax.sharding import PartitionSpec as P

KVH = 8
HD = 64
L_MAX = 128
P_SIZE = 256


THETA = 10000000.0
EPSILON = 1e-05


def rms_scale(wide, gain):
    mean_square = jnp.mean(wide * wide, axis=-1, keepdims=True)
    return (wide * lax.rsqrt(mean_square + EPSILON) * gain.astype(jnp.float32)).astype(jnp.bfloat16)


def rotate(vectors, positions):
    half = HD // 2
    freqs = THETA ** (-(jnp.arange(half, dtype=jnp.float32) * 2.0 / HD))
    angles = positions[:, None] * freqs[None, :]
    cosine = jnp.cos(angles)
    sine = jnp.sin(angles)
    first = vectors[..., :half]
    second = vectors[..., half:]
    return jnp.concatenate(
        [first * cosine - second * sine, second * cosine + first * sine], axis=-1
    )


def layer(
    suffix_states,
    suffix_lengths,
    request_group,
    group_owner,
    request_order,
    prefix_cache,
    norm_attn,
    w_query,
    w_key,
    w_value,
    w_out,
    norm_mlp,
    w_gate,
    w_up,
    w_down,
):
    dp_count = lax.axis_size("dp")
    tp_count = lax.axis_size("tensor")
    dp_index = lax.axis_index("dp")
    tp_index = lax.axis_index("tensor")
    total_reqs = suffix_lengths.shape[0]
    local_reqs = total_reqs // dp_count
    row_count = local_reqs * L_MAX
    heads_here = w_query.shape[1] // HD
    assert heads_here == 1 and local_reqs == 2
    kv_cols = w_key.shape[1]
    d_here = kv_cols // KVH
    score_scale = HD ** (-0.5)

    slot_hit = (
        request_order[:, None] == jnp.arange(suffix_states.shape[0], dtype=jnp.int32)[None, :]
    ).astype(jnp.bfloat16)
    routed = jnp.dot(
        slot_hit, suffix_states.reshape(suffix_states.shape[0], -1), preferred_element_type=jnp.float32
    ).astype(jnp.bfloat16).reshape(suffix_states.shape)
    pos_here = routed.shape[1]
    width_here = routed.shape[2]
    state_part = routed.reshape(dp_count, local_reqs * pos_here * width_here)
    prefix_flat = prefix_cache.reshape(1, -1)
    prefix_part = jnp.broadcast_to(prefix_flat, (dp_count, prefix_flat.shape[1]))
    first = lax.all_to_all(
        jnp.concatenate([state_part, prefix_part], axis=1), "dp", 0, 0, tiled=True
    )
    state_split = state_part.shape[1]
    routed_here = (
        first[:, :state_split]
        .reshape(dp_count, local_reqs, pos_here, width_here)
        .transpose(1, 0, 2, 3)
        .reshape(local_reqs, dp_count * pos_here, width_here)
    )
    prefix_rows = prefix_cache.shape[1]
    prefix_all = first[:, state_split:].reshape(dp_count, prefix_rows, KVH, 2 * HD)

    state_shard = routed_here.reshape(row_count, width_here)
    req_ids = lax.dynamic_slice_in_dim(request_order, dp_index * local_reqs, local_reqs)
    hit = jnp.arange(total_reqs, dtype=jnp.int32)[None, :] == req_ids[:, None]
    lengths_here = jnp.sum(jnp.where(hit, suffix_lengths[None, :], 0), axis=1)
    group_here = jnp.sum(jnp.where(hit, request_group[:, 0][None, :], 0), axis=1)
    group_hit = jnp.arange(group_owner.shape[0], dtype=jnp.int32)[None, :] == group_here[:, None]
    owner_here = jnp.sum(jnp.where(group_hit, group_owner[None, :], 0), axis=1)
    position = jnp.arange(L_MAX, dtype=jnp.int32)
    valid = (position[None, :] < lengths_here[:, None]).reshape(row_count)
    positions = (P_SIZE + position).astype(jnp.float32)

    core = tp_index % 2
    pair = [(t, t ^ 1) for t in range(tp_count)]
    q_cols = w_query.shape[1]
    w_qkv_sib = lax.ppermute(jnp.concatenate([w_query, w_key, w_value], axis=1), "tensor", pair)
    w_query_chip = jnp.concatenate([w_query, w_qkv_sib[:, :q_cols]], axis=1)
    w_key_chip = jnp.concatenate([w_key, w_qkv_sib[:, q_cols : q_cols + kv_cols]], axis=1)
    w_value_chip = jnp.concatenate([w_value, w_qkv_sib[:, q_cols + kv_cols :]], axis=1)

    per_kv = tp_count // KVH
    chosen = jnp.stack(
        [lax.dynamic_index_in_dim(prefix_all, owner_here[r], 0, keepdims=False) for r in range(local_reqs)]
    ).transpose(2, 0, 1, 3)
    chosen = jnp.broadcast_to(
        chosen[:, None], (KVH, per_kv // local_reqs) + chosen.shape[1:]
    ).reshape(tp_count, prefix_rows, 2 * HD)

    state_req = routed_here
    sent = jnp.tile(state_req, (tp_count // 2, 1, 1))
    got = lax.all_to_all(sent, "tensor", 0, 0, tiled=True)
    full_rows = got.transpose(1, 0, 2).reshape(L_MAX, tp_count * width_here)
    normed = rms_scale(full_rows.astype(jnp.float32), norm_attn)
    query = jnp.dot(normed, w_query_chip, preferred_element_type=jnp.float32)
    query = query.reshape(L_MAX, 2 * heads_here, HD).transpose(1, 0, 2)
    query = rotate(query, positions).astype(jnp.bfloat16)
    kv_part = jnp.dot(
        normed, jnp.concatenate([w_key_chip, w_value_chip], axis=1), preferred_element_type=jnp.float32
    ).astype(jnp.bfloat16)
    chip_d = 2 * d_here
    kv_sent = kv_part.reshape(L_MAX, 4, d_here, KVH).transpose(3, 0, 1, 2).reshape(KVH, L_MAX, 2 * chip_d)
    kv_sent = jnp.broadcast_to(kv_sent[:, None], (KVH, per_kv, L_MAX, 2 * chip_d)).reshape(
        tp_count, L_MAX, 2 * chip_d
    )
    prefix_split = chosen.shape[1] * chosen.shape[2]
    packed = jnp.concatenate([chosen.reshape(tp_count, -1), kv_sent.reshape(tp_count, -1)], axis=1)
    both = lax.all_to_all(packed, "tensor", 0, 0, tiled=True)
    picked = both[:, :prefix_split].reshape(tp_count, prefix_rows, 2 * HD)
    picked = picked.reshape(tp_count * prefix_rows, 2 * HD)
    prefix_keys = picked[:, :HD]
    prefix_values = picked[:, HD:]
    kv_got = both[:, prefix_split:].reshape(tp_count // 2, 2, L_MAX, 2 * chip_d)
    kv_got = lax.dynamic_index_in_dim(kv_got, core, 1, keepdims=False)
    keys4 = kv_got[:, :, : 2 * d_here].reshape(tp_count // 2, L_MAX, 2, d_here)
    vals4 = kv_got[:, :, 2 * d_here :].reshape(tp_count // 2, L_MAX, 2, d_here)
    flip = core == 1
    keys4 = jnp.where(flip, keys4[:, :, ::-1], keys4)
    vals4 = jnp.where(flip, vals4[:, :, ::-1], vals4)
    key_raw = keys4.transpose(1, 0, 2, 3).reshape(L_MAX, HD)
    value = vals4.transpose(1, 0, 2, 3).reshape(L_MAX, HD)
    key_rot = rotate(key_raw.astype(jnp.float32), positions).astype(jnp.bfloat16)

    out_width = kv_cols
    out_first = (tp_index * out_width) % HD
    sib_first = ((tp_index ^ 1) * out_width) % HD
    kv_for_sib = jnp.concatenate(
        [lax.dynamic_slice_in_dim(key_rot, sib_first, out_width, 1),
         lax.dynamic_slice_in_dim(value, sib_first, out_width, 1)], axis=1
    )
    kv_from_sib = lax.ppermute(kv_for_sib, "tensor", pair)
    kv_mine = jnp.concatenate(
        [lax.dynamic_slice_in_dim(key_rot, out_first, out_width, 1),
         lax.dynamic_slice_in_dim(value, out_first, out_width, 1)], axis=1
    )
    kv_two = jnp.where(
        core == 0, jnp.stack([kv_mine, kv_from_sib]), jnp.stack([kv_from_sib, kv_mine])
    )
    valid3 = valid.reshape(local_reqs, L_MAX, 1)
    keys_out = jnp.where(valid3, kv_two[:, :, :out_width], 0.0).astype(jnp.bfloat16)
    values_out = jnp.where(valid3, kv_two[:, :, out_width:], 0.0).astype(jnp.bfloat16)

    length_me = lax.dynamic_index_in_dim(lengths_here, core, 0, keepdims=False)
    prefix_scores = jnp.einsum(
        "htd,pd->htp", query, prefix_keys, preferred_element_type=jnp.float32
    ) * score_scale
    self_scores = jnp.einsum(
        "htd,sd->hts", query, key_rot, preferred_element_type=jnp.float32
    ) * score_scale
    self_allowed = (position[None, None, :] <= position[None, :, None]) & (
        position[None, None, :] < length_me
    )
    scores = jnp.concatenate([prefix_scores, self_scores], axis=2)
    allowed = jnp.concatenate(
        [jnp.ones(prefix_scores.shape, bool), jnp.broadcast_to(self_allowed, self_scores.shape)], axis=2
    )
    row_peak = jnp.max(jnp.where(allowed, scores, -jnp.inf), axis=2, keepdims=True)
    weights = jnp.where(allowed, jnp.exp(scores - row_peak), 0.0)
    total = jnp.sum(weights, axis=2, keepdims=True)
    all_values = jnp.concatenate([prefix_values, value], axis=0)
    numerator = jnp.einsum(
        "htk,kd->htd", weights.astype(jnp.bfloat16), all_values, preferred_element_type=jnp.float32
    )
    attention = (numerator / total).astype(jnp.bfloat16).transpose(1, 0, 2).reshape(L_MAX, 2 * HD)

    w_out_sib = lax.ppermute(w_out, "tensor", pair)
    w_out_chip = jnp.concatenate([w_out, w_out_sib], axis=0)
    attn_terms = jnp.dot(attention, w_out_chip, preferred_element_type=jnp.float32)
    sent = attn_terms.astype(jnp.bfloat16).reshape(L_MAX, tp_count, width_here).transpose(1, 0, 2)
    got = lax.all_to_all(sent, "tensor", 0, 0, tiled=True)
    attn_share = jnp.sum(
        got.reshape(tp_count // 2, local_reqs, L_MAX, width_here).astype(jnp.float32), axis=0
    ).reshape(row_count, width_here)
    middle = (state_shard.astype(jnp.float32) + attn_share).astype(jnp.bfloat16)
    w_gu_sib, w_down_sib = lax.ppermute(
        (jnp.concatenate([w_gate, w_up], axis=1), w_down), "tensor", pair
    )
    units = w_gate.shape[1]
    w_gate_chip = jnp.concatenate([w_gate, w_gu_sib[:, :units]], axis=1)
    w_up_chip = jnp.concatenate([w_up, w_gu_sib[:, units:]], axis=1)
    w_down_chip = jnp.concatenate([w_down, w_down_sib], axis=0)
    middle_req = middle.reshape(local_reqs, L_MAX, width_here)
    sent = jnp.tile(middle_req, (tp_count // 2, 1, 1))
    got = lax.all_to_all(sent, "tensor", 0, 0, tiled=True)
    middle_rows = got.transpose(1, 0, 2).reshape(L_MAX, tp_count * width_here)
    normed_two = rms_scale(middle_rows.astype(jnp.float32), norm_mlp)
    gate = jnp.dot(normed_two, w_gate_chip, preferred_element_type=jnp.float32)
    upper = jnp.dot(normed_two, w_up_chip, preferred_element_type=jnp.float32)
    hidden = (jax.nn.silu(gate) * upper).astype(jnp.bfloat16)
    down_terms = jnp.dot(hidden, w_down_chip, preferred_element_type=jnp.float32)
    sent = down_terms.astype(jnp.bfloat16).reshape(L_MAX, tp_count, width_here).transpose(1, 0, 2)
    got = lax.all_to_all(sent, "tensor", 0, 0, tiled=True)
    down_share = jnp.sum(
        got.reshape(tp_count // 2, local_reqs, L_MAX, width_here).astype(jnp.float32), axis=0
    ).reshape(row_count, width_here)
    result = middle.astype(jnp.float32) + down_share
    result = (
        jnp.where(valid[:, None], result, 0.0)
        .astype(jnp.bfloat16)
        .reshape(local_reqs, L_MAX, width_here)
    )
    returned = lax.all_to_all(result, "dp", split_axis=1, concat_axis=0, tiled=True)
    order_hit = (
        jnp.arange(total_reqs, dtype=jnp.int32)[:, None] == request_order[None, :]
    ).astype(jnp.bfloat16)
    hidden_out = jnp.dot(
        order_hit, returned.reshape(total_reqs, -1), preferred_element_type=jnp.float32
    ).astype(jnp.bfloat16).reshape(returned.shape)
    return (hidden_out, keys_out, values_out)


def solution(mesh):
    in_specs = (
        P(None, "dp", "tensor"),
        P(),
        P(),
        P(),
        P(),
        P("dp", "tensor", None),
        P(),
        P(None, "tensor"),
        P(None, "tensor"),
        P(None, "tensor"),
        P("tensor", None),
        P(),
        P(None, "tensor"),
        P(None, "tensor"),
        P("tensor", None),
    )
    out_specs = (P(None, "dp", "tensor"), P("dp", None, "tensor"), P("dp", None, "tensor"))
    return jax.shard_map(layer, mesh=mesh, in_specs=in_specs, out_specs=out_specs, check_vma=False)
```

```python
import jax
import jax.numpy as jnp
from jax import lax
from jax.sharding import PartitionSpec as P

KVH = 8
HD = 64
L_MAX = 128
P_SIZE = 256


THETA = 10000000.0
EPSILON = 1e-05


def rms_scale(wide, gain):
    mean_square = jnp.mean(wide * wide, axis=-1, keepdims=True)
    return (wide * lax.rsqrt(mean_square + EPSILON) * gain.astype(jnp.float32)).astype(jnp.bfloat16)


def rotate(vectors, positions):
    half = HD // 2
    freqs = THETA ** (-(jnp.arange(half, dtype=jnp.float32) * 2.0 / HD))
    angles = positions[:, None] * freqs[None, :]
    cosine = jnp.cos(angles)
    sine = jnp.sin(angles)
    first = vectors[..., :half]
    second = vectors[..., half:]
    return jnp.concatenate(
        [first * cosine - second * sine, second * cosine + first * sine], axis=-1
    )


def layer(
    suffix_states,
    suffix_lengths,
    request_group,
    group_owner,
    request_order,
    prefix_cache,
    norm_attn,
    w_query,
    w_key,
    w_value,
    w_out,
    norm_mlp,
    w_gate,
    w_up,
    w_down,
):
    dp_count = lax.axis_size("dp")
    tp_count = lax.axis_size("tensor")
    dp_index = lax.axis_index("dp")
    tp_index = lax.axis_index("tensor")
    total_reqs = suffix_lengths.shape[0]
    local_reqs = total_reqs // dp_count
    row_count = local_reqs * L_MAX
    heads_here = w_query.shape[1] // HD
    assert heads_here == 1 and local_reqs == 2
    kv_cols = w_key.shape[1]
    d_here = kv_cols // KVH
    score_scale = HD ** (-0.5)

    slot_hit = (
        request_order[:, None] == jnp.arange(suffix_states.shape[0], dtype=jnp.int32)[None, :]
    ).astype(jnp.bfloat16)
    routed = jnp.dot(
        slot_hit, suffix_states.reshape(suffix_states.shape[0], -1), preferred_element_type=jnp.float32
    ).astype(jnp.bfloat16).reshape(suffix_states.shape)
    pos_here = routed.shape[1]
    width_here = routed.shape[2]
    state_part = routed.reshape(dp_count, local_reqs * pos_here * width_here)
    prefix_flat = prefix_cache.reshape(1, -1)
    prefix_part = jnp.broadcast_to(prefix_flat, (dp_count, prefix_flat.shape[1]))
    first = lax.all_to_all(
        jnp.concatenate([state_part, prefix_part], axis=1), "dp", 0, 0, tiled=True
    )
    state_split = state_part.shape[1]
    routed_here = (
        first[:, :state_split]
        .reshape(dp_count, local_reqs, pos_here, width_here)
        .transpose(1, 0, 2, 3)
        .reshape(local_reqs, dp_count * pos_here, width_here)
    )
    prefix_rows = prefix_cache.shape[1]
    prefix_all = first[:, state_split:].reshape(dp_count, prefix_rows, KVH, 2 * HD)

    state_shard = routed_here.reshape(row_count, width_here)
    req_ids = lax.dynamic_slice_in_dim(request_order, dp_index * local_reqs, local_reqs)
    hit = jnp.arange(total_reqs, dtype=jnp.int32)[None, :] == req_ids[:, None]
    lengths_here = jnp.sum(jnp.where(hit, suffix_lengths[None, :], 0), axis=1)
    group_here = jnp.sum(jnp.where(hit, request_group[:, 0][None, :], 0), axis=1)
    group_hit = jnp.arange(group_owner.shape[0], dtype=jnp.int32)[None, :] == group_here[:, None]
    owner_here = jnp.sum(jnp.where(group_hit, group_owner[None, :], 0), axis=1)
    position = jnp.arange(L_MAX, dtype=jnp.int32)
    valid = (position[None, :] < lengths_here[:, None]).reshape(row_count)
    positions = (P_SIZE + position).astype(jnp.float32)

    core = tp_index % 2
    pair = [(t, t ^ 1) for t in range(tp_count)]
    q_cols = w_query.shape[1]
    w_qkv_sib = lax.ppermute(jnp.concatenate([w_query, w_key, w_value], axis=1), "tensor", pair)
    w_query_chip = jnp.concatenate([w_query, w_qkv_sib[:, :q_cols]], axis=1)
    w_key_chip = jnp.concatenate([w_key, w_qkv_sib[:, q_cols : q_cols + kv_cols]], axis=1)
    w_value_chip = jnp.concatenate([w_value, w_qkv_sib[:, q_cols + kv_cols :]], axis=1)

    per_kv = tp_count // KVH
    chosen = jnp.stack(
        [lax.dynamic_index_in_dim(prefix_all, owner_here[r], 0, keepdims=False) for r in range(local_reqs)]
    ).transpose(2, 0, 1, 3)
    chosen = jnp.broadcast_to(
        chosen[:, None], (KVH, per_kv // local_reqs) + chosen.shape[1:]
    ).reshape(tp_count, prefix_rows, 2 * HD)

    state_req = routed_here
    sent = jnp.tile(state_req, (tp_count // 2, 1, 1))
    got = lax.all_to_all(sent, "tensor", 0, 0, tiled=True)
    full_rows = got.transpose(1, 0, 2).reshape(L_MAX, tp_count * width_here)
    normed = rms_scale(full_rows.astype(jnp.float32), norm_attn)
    query = jnp.dot(normed, w_query_chip, preferred_element_type=jnp.float32)
    query = query.reshape(L_MAX, 2 * heads_here, HD).transpose(1, 0, 2)
    query = rotate(query, positions).astype(jnp.bfloat16)
    kv_part = jnp.dot(
        normed, jnp.concatenate([w_key_chip, w_value_chip], axis=1), preferred_element_type=jnp.float32
    ).astype(jnp.bfloat16)
    chip_d = 2 * d_here
    kv_sent = kv_part.reshape(L_MAX, 4, d_here, KVH).transpose(3, 0, 1, 2).reshape(KVH, L_MAX, 2 * chip_d)
    kv_sent = jnp.broadcast_to(kv_sent[:, None], (KVH, per_kv, L_MAX, 2 * chip_d)).reshape(
        tp_count, L_MAX, 2 * chip_d
    )
    prefix_split = chosen.shape[1] * chosen.shape[2]
    packed = jnp.concatenate([chosen.reshape(tp_count, -1), kv_sent.reshape(tp_count, -1)], axis=1)
    both = lax.all_to_all(packed, "tensor", 0, 0, tiled=True)
    picked = both[:, :prefix_split].reshape(tp_count, prefix_rows, 2 * HD)
    picked = picked.reshape(tp_count * prefix_rows, 2 * HD)
    prefix_keys = picked[:, :HD]
    prefix_values = picked[:, HD:]
    kv_got = both[:, prefix_split:].reshape(tp_count // 2, 2, L_MAX, 2 * chip_d)
    kv_got = jnp.take(kv_got, core, axis=1)
    keys4 = kv_got[:, :, : 2 * d_here].reshape(tp_count // 2, L_MAX, 2, d_here)
    vals4 = kv_got[:, :, 2 * d_here :].reshape(tp_count // 2, L_MAX, 2, d_here)
    flip = core == 1
    keys4 = jnp.where(flip, keys4[:, :, ::-1], keys4)
    vals4 = jnp.where(flip, vals4[:, :, ::-1], vals4)
    key_raw = keys4.transpose(1, 0, 2, 3).reshape(L_MAX, HD)
    value = vals4.transpose(1, 0, 2, 3).reshape(L_MAX, HD)
    key_rot = rotate(key_raw.astype(jnp.float32), positions).astype(jnp.bfloat16)

    out_width = kv_cols
    out_first = (tp_index * out_width) % HD
    sib_first = ((tp_index ^ 1) * out_width) % HD
    kv_for_sib = jnp.concatenate(
        [lax.dynamic_slice_in_dim(key_rot, sib_first, out_width, 1),
         lax.dynamic_slice_in_dim(value, sib_first, out_width, 1)], axis=1
    )
    kv_from_sib = lax.ppermute(kv_for_sib, "tensor", pair)
    kv_mine = jnp.concatenate(
        [lax.dynamic_slice_in_dim(key_rot, out_first, out_width, 1),
         lax.dynamic_slice_in_dim(value, out_first, out_width, 1)], axis=1
    )
    kv_two = jnp.where(
        core == 0, jnp.stack([kv_mine, kv_from_sib]), jnp.stack([kv_from_sib, kv_mine])
    )
    valid3 = valid.reshape(local_reqs, L_MAX, 1)
    keys_out = jnp.where(valid3, kv_two[:, :, :out_width], 0.0).astype(jnp.bfloat16)
    values_out = jnp.where(valid3, kv_two[:, :, out_width:], 0.0).astype(jnp.bfloat16)

    length_me = jnp.take(lengths_here, core)
    prefix_scores = jnp.einsum(
        "htd,pd->htp", query, prefix_keys, preferred_element_type=jnp.float32
    ) * score_scale
    self_scores = jnp.einsum(
        "htd,sd->hts", query, key_rot, preferred_element_type=jnp.float32
    ) * score_scale
    self_allowed = (position[None, None, :] <= position[None, :, None]) & (
        position[None, None, :] < length_me
    )
    scores = jnp.concatenate([prefix_scores, self_scores], axis=2)
    allowed = jnp.concatenate(
        [jnp.ones(prefix_scores.shape, bool), jnp.broadcast_to(self_allowed, self_scores.shape)], axis=2
    )
    row_peak = jnp.max(jnp.where(allowed, scores, -jnp.inf), axis=2, keepdims=True)
    weights = jnp.where(allowed, jnp.exp(scores - row_peak), 0.0)
    total = jnp.sum(weights, axis=2, keepdims=True)
    all_values = jnp.concatenate([prefix_values, value], axis=0)
    numerator = jnp.einsum(
        "htk,kd->htd", weights.astype(jnp.bfloat16), all_values, preferred_element_type=jnp.float32
    )
    attention = (numerator / total).astype(jnp.bfloat16).transpose(1, 0, 2).reshape(L_MAX, 2 * HD)

    w_out_sib = lax.ppermute(w_out, "tensor", pair)
    w_out_chip = jnp.concatenate([w_out, w_out_sib], axis=0)
    attn_terms = jnp.dot(attention, w_out_chip, preferred_element_type=jnp.float32)
    sent = attn_terms.astype(jnp.bfloat16).reshape(L_MAX, tp_count, width_here).transpose(1, 0, 2)
    got = lax.all_to_all(sent, "tensor", 0, 0, tiled=True)
    attn_share = jnp.sum(
        got.reshape(tp_count // 2, local_reqs, L_MAX, width_here).astype(jnp.float32), axis=0
    ).reshape(row_count, width_here)
    middle = (state_shard.astype(jnp.float32) + attn_share).astype(jnp.bfloat16)
    w_gu_sib, w_down_sib = lax.ppermute(
        (jnp.concatenate([w_gate, w_up], axis=1), w_down), "tensor", pair
    )
    units = w_gate.shape[1]
    w_gate_chip = jnp.concatenate([w_gate, w_gu_sib[:, :units]], axis=1)
    w_up_chip = jnp.concatenate([w_up, w_gu_sib[:, units:]], axis=1)
    w_down_chip = jnp.concatenate([w_down, w_down_sib], axis=0)
    middle_req = middle.reshape(local_reqs, L_MAX, width_here)
    sent = jnp.tile(middle_req, (tp_count // 2, 1, 1))
    got = lax.all_to_all(sent, "tensor", 0, 0, tiled=True)
    middle_rows = got.transpose(1, 0, 2).reshape(L_MAX, tp_count * width_here)
    normed_two = rms_scale(middle_rows.astype(jnp.float32), norm_mlp)
    gate = jnp.dot(normed_two, w_gate_chip, preferred_element_type=jnp.float32)
    upper = jnp.dot(normed_two, w_up_chip, preferred_element_type=jnp.float32)
    hidden = (jax.nn.silu(gate) * upper).astype(jnp.bfloat16)
    down_terms = jnp.dot(hidden, w_down_chip, preferred_element_type=jnp.float32)
    sent = down_terms.astype(jnp.bfloat16).reshape(L_MAX, tp_count, width_here).transpose(1, 0, 2)
    got = lax.all_to_all(sent, "tensor", 0, 0, tiled=True)
    down_share = jnp.sum(
        got.reshape(tp_count // 2, local_reqs, L_MAX, width_here).astype(jnp.float32), axis=0
    ).reshape(row_count, width_here)
    result = middle.astype(jnp.float32) + down_share
    result = (
        jnp.where(valid[:, None], result, 0.0)
        .astype(jnp.bfloat16)
        .reshape(local_reqs, L_MAX, width_here)
    )
    returned = lax.all_to_all(result, "dp", split_axis=1, concat_axis=0, tiled=True)
    order_hit = (
        jnp.arange(total_reqs, dtype=jnp.int32)[:, None] == request_order[None, :]
    ).astype(jnp.bfloat16)
    hidden_out = jnp.einsum(
        "rs,spf->rpf", order_hit, returned, preferred_element_type=jnp.float32
    ).astype(jnp.bfloat16)
    return (hidden_out, keys_out, values_out)


def solution(mesh):
    in_specs = (
        P(None, "dp", "tensor"),
        P(),
        P(),
        P(),
        P(),
        P("dp", "tensor", None),
        P(),
        P(None, "tensor"),
        P(None, "tensor"),
        P(None, "tensor"),
        P("tensor", None),
        P(),
        P(None, "tensor"),
        P(None, "tensor"),
        P("tensor", None),
    )
    out_specs = (P(None, "dp", "tensor"), P("dp", None, "tensor"), P("dp", None, "tensor"))
    return jax.shard_map(layer, mesh=mesh, in_specs=in_specs, out_specs=out_specs, check_vma=False)
```
